128 devices in a mesh: row: 8 (over y, core), col: 16 (over z, x).
Axes of the slice: x: 4, y: 4, z: 4, core: 2. Of those that a mesh axis runs over, the one named last changes fastest.
Arguments:
- constraint_features: bfloat16 [32768, 768], P(('row', 'col')), may hold values from -6 to 6
- variable_features: bfloat16 [32768, 768], P(('row', 'col')), may hold values from -6 to 6
- variable_cotangent: bfloat16 [32768, 768], P(('row', 'col')), may hold values from -6 to 6
- constraint_weight: bfloat16 [768, 768], replicated, may hold values from -0.21875 to 0.21875
- variable_weight: bfloat16 [768, 768], replicated, may hold values from -0.21875 to 0.21875
- bias: float32 [768], replicated, may hold values from -4 to 4
- send_rows: int32 [2, 128, 512], P(None, ('row', 'col')), may hold values from 0 to 255
- recv_count: int32 [2, 128, 128], P(None, ('row', 'col')), may hold values from 2 to 4, as said below
- edge_slots: int32 [2, 262144], P(None, ('row', 'col')), may hold values from 0 to 511
Outputs:
- grad_con: bfloat16 [32768, 768], P(('row', 'col'))
- grad_var: bfloat16 [32768, 768], P(('row', 'col'))
- grad_wcon: float32 [768, 768], P(('row', 'col'))
- grad_wvar: float32 [768, 768], P(('row', 'col'))
- grad_bias: float32 [768], P(('row', 'col'))
The draws below stay inside these ranges and needn't reach their ends.
Inputs may be any that keep to these rules, and one draw needn't show every extreme that they name: `recv_count`: every device holds exactly 4 live slots from some peer, for each side.
All inputs are finite; a program needn't handle non-finite values.
Results may differ from the reference program's by a relative error of at most 0.0063.
Values may be sent and summed in bfloat16 or wider, within the bound.
No kernel may reach another device: no remote copies, remote signals or barrier semaphores. Data moves between devices by JAX's collectives and lax.ppermute only.
A program may use at most 128 MiB of HBM per device.

```python
import jax
import jax.numpy as jnp
from jax import lax

D = 768
MASTERS_DEV = 256
SLOT_CAP = 4
EDGES_DEV = 2048
MASTERS = 32768
MIRRORS = 512
EDGES = 262144
DEVICES = 128


def draw_recv_count(key, part):
    base = jax.random.randint(key, (2, DEVICES, DEVICES), SLOT_CAP // 2, SLOT_CAP + 1)
    picked = jax.random.randint(jax.random.fold_in(key, 7), (2, DEVICES, 1), 0, DEVICES)
    column = jnp.arange(DEVICES, dtype=jnp.int32)[None, None, :]
    return jnp.where(column == picked, SLOT_CAP, base).astype(jnp.int32)


def with_ends(entries, own_key, low, high):
    longest = entries.shape.index(max(entries.shape))
    spots = []
    for shift in (0, 1):
        where = [jax.random.randint(jax.random.fold_in(own_key, axis), (), 0, length) for axis, length in enumerate(entries.shape)]
        where[longest] = (where[longest] + shift) % entries.shape[longest]
        spots.append(tuple(where))
    return entries.at[spots[0]].set(low).at[spots[1]].set(high)


def block_levels(key, extent, cuts, smallest, high):
    factor_of = 1.0
    for position, parts in cuts:
        heights = jax.random.uniform(jax.random.fold_in(jax.random.fold_in(key, 6), position), (parts,), jnp.float32, smallest / len(cuts), high / len(cuts))
        factor_of = factor_of * jnp.repeat(jnp.exp(heights), extent[position] // parts).reshape((-1,) + (1,) * (len(extent) - 1 - position))
    return factor_of


def bell_draw(key, dims, scale, most, cuts=(), held_as=jnp.bfloat16):
    level = block_levels(key, dims, cuts, -0.22, 0.18) if cuts else 1.0
    result = jax.random.normal(key, dims, jnp.float32) * scale * level
    return jnp.minimum(jnp.maximum(result, -most), most).astype(held_as)


def setup_inputs(seed: int = 0) -> dict:
    keys = jax.random.split(jax.random.key(seed), 10)
    return {
        "constraint_features": bell_draw(keys[0], (MASTERS, D), 1.0, 6.0, ((0, 128),)),
        "variable_features": bell_draw(keys[1], (MASTERS, D), 1.0, 6.0, ((0, 128),)),
        "variable_cotangent": bell_draw(keys[2], (MASTERS, D), 1.0, 6.0, ((0, 128),)),
        "constraint_weight": bell_draw(keys[3], (D, D), D ** -0.5, 0.21875),
        "variable_weight": bell_draw(keys[4], (D, D), D ** -0.5, 0.21875),
        "bias": bell_draw(keys[5], (D,), 0.7, 4.0, (), jnp.float32),
        "send_rows": with_ends(jax.random.randint(keys[6], (2, DEVICES, MIRRORS), 0, MASTERS_DEV), jax.random.fold_in(keys[6], 1), 0, MASTERS_DEV - 1).astype(jnp.int32),
        "recv_count": draw_recv_count(jax.random.fold_in(keys[9], 71), 0),
        "edge_slots": with_ends(jax.random.randint(keys[8], (2, EDGES), 0, MIRRORS), jax.random.fold_in(keys[8], 1), 0, MIRRORS - 1).astype(jnp.int32),
    }


def per_device_terms(constraint_mirror_rows, variable_mirror_rows, cotangent_mirror_rows, edge_positions, edge_active_mask, constraint_weight, variable_weight, bias):
    constraint_projection = jnp.dot(constraint_mirror_rows, constraint_weight, preferred_element_type=jnp.float32)
    variable_projection = jnp.dot(variable_mirror_rows, variable_weight, preferred_element_type=jnp.float32)
    pre_act = constraint_projection[edge_positions[0]] + variable_projection[edge_positions[1]] + bias.astype(jnp.float32)[None, :]
    sigmoid_pre = jax.nn.sigmoid(pre_act)
    message_derivative = sigmoid_pre * (1.0 + pre_act * (1.0 - sigmoid_pre))
    edge_delta = (cotangent_mirror_rows[edge_positions[1]].astype(jnp.float32) * message_derivative * edge_active_mask[:, None]).astype(jnp.bfloat16)
    replica_rows = constraint_mirror_rows.shape[0]
    constraint_projection_gradient = jax.ops.segment_sum(edge_delta.astype(jnp.float32), edge_positions[0], replica_rows).astype(jnp.bfloat16)
    variable_projection_gradient = jax.ops.segment_sum(edge_delta.astype(jnp.float32), edge_positions[1], replica_rows).astype(jnp.bfloat16)
    back_con = jnp.dot(constraint_projection_gradient, constraint_weight.T, preferred_element_type=jnp.float32).astype(jnp.bfloat16)
    back_var = jnp.dot(variable_projection_gradient, variable_weight.T, preferred_element_type=jnp.float32).astype(jnp.bfloat16)
    constraint_term = jnp.dot(constraint_mirror_rows.T, constraint_projection_gradient, preferred_element_type=jnp.float32)
    variable_term = jnp.dot(variable_mirror_rows.T, variable_projection_gradient, preferred_element_type=jnp.float32)
    term_bias = jnp.sum(edge_delta.astype(jnp.float32), axis=0)
    return back_con, back_var, constraint_term, variable_term, term_bias


def reference(constraint_features, variable_features, variable_cotangent, constraint_weight, variable_weight, bias, send_rows, recv_count, edge_slots):
    owner_base = (jnp.arange(DEVICES, dtype=jnp.int32) * MASTERS_DEV)[None, :, None]
    global_rows = (send_rows + owner_base).reshape(2, DEVICES, DEVICES, SLOT_CAP)
    global_rows = global_rows.transpose(0, 2, 1, 3).reshape(2, DEVICES, MIRRORS)
    slot_pos = jnp.arange(MIRRORS, dtype=jnp.int32) % SLOT_CAP
    slots_all = edge_slots.reshape(2, DEVICES, EDGES_DEV).transpose(1, 0, 2)
    counts_all = recv_count.transpose(1, 0, 2)
    rows_all = global_rows.transpose(1, 0, 2)

    def one_device(carry, inputs):
        resident_rows, resident_positions, counts_here = inputs
        constraint_mirror_rows = constraint_features[resident_rows[0]]
        variable_mirror_rows = variable_features[resident_rows[1]]
        cotangent_mirror_rows = variable_cotangent[resident_rows[1]]
        slot_live = slot_pos[None, :] < jnp.repeat(counts_here, SLOT_CAP, axis=1)
        edge_active_mask = jnp.where(slot_live[0][resident_positions[0]] & slot_live[1][resident_positions[1]], 1.0, 0.0).astype(jnp.float32)
        back_con, back_var, constraint_term, variable_term, term_bias = per_device_terms(
            constraint_mirror_rows, variable_mirror_rows, cotangent_mirror_rows, resident_positions, edge_active_mask, constraint_weight, variable_weight, bias)
        carry = (carry[0] + constraint_term, carry[1] + variable_term, carry[2] + term_bias)
        return carry, (back_con, back_var)

    start = (jnp.zeros((D, D), jnp.float32), jnp.zeros((D, D), jnp.float32), jnp.zeros((D,), jnp.float32))
    sums, backs = lax.scan(one_device, start, (rows_all, slots_all, counts_all))
    grad_con = jax.ops.segment_sum(backs[0].reshape(-1, D).astype(jnp.float32), global_rows[0].reshape(-1), MASTERS)
    grad_var = jax.ops.segment_sum(backs[1].reshape(-1, D).astype(jnp.float32), global_rows[1].reshape(-1), MASTERS)
    grad_var = variable_cotangent.astype(jnp.float32) + grad_var
    factor = float(DEVICES * EDGES_DEV) ** -0.5
    return (grad_con.astype(jnp.bfloat16), grad_var.astype(jnp.bfloat16),
            sums[0] * factor, sums[1] * factor, sums[2] * factor)
```

```python
import jax
import jax.numpy as jnp
from jax import lax
from jax.sharding import PartitionSpec as P


def one_hot_table(indices, width):
    columns = lax.broadcasted_iota(jnp.int32, (indices.shape[0], width), 1)
    return jnp.where(columns == indices[:, None], 1.0, 0.0).astype(jnp.bfloat16)


def pick_rows(table, values):
    return jnp.dot(table, values, preferred_element_type=jnp.float32).astype(jnp.bfloat16)


def on_device(
    constraint_features,
    variable_features,
    variable_cotangent,
    constraint_weight,
    variable_weight,
    bias,
    send_rows,
    recv_count,
    edge_slots,
):
    device_count = lax.axis_size(("row", "col"))
    slot_cap = send_rows.shape[2] // device_count
    embedding_width = constraint_features.shape[1]
    replica_rows = device_count * slot_cap
    master_rows = constraint_features.shape[0]
    select_con = one_hot_table(send_rows[0, 0], master_rows)
    select_var = one_hot_table(send_rows[1, 0], master_rows)
    out_con = pick_rows(select_con, constraint_features).reshape(
        device_count, slot_cap, embedding_width
    )
    out_var = pick_rows(select_var, variable_features).reshape(
        device_count, slot_cap, embedding_width
    )
    out_cot = pick_rows(select_var, variable_cotangent).reshape(
        device_count, slot_cap, embedding_width
    )
    constraint_mirror_rows, variable_mirror_rows, cotangent_mirror_rows = (
        lax.all_to_all(out_con, ("row", "col"), split_axis=0, concat_axis=0, tiled=True),
        lax.all_to_all(out_var, ("row", "col"), split_axis=0, concat_axis=0, tiled=True),
        lax.all_to_all(out_cot, ("row", "col"), split_axis=0, concat_axis=0, tiled=True),
    )
    constraint_mirror_rows = constraint_mirror_rows.reshape(replica_rows, embedding_width)
    variable_mirror_rows = variable_mirror_rows.reshape(replica_rows, embedding_width)
    cotangent_mirror_rows = cotangent_mirror_rows.reshape(replica_rows, embedding_width)
    slot_pos = lax.broadcasted_iota(jnp.int32, (2, replica_rows), 1) % slot_cap
    slot_live = jnp.where(
        slot_pos < jnp.repeat(recv_count[:, 0], slot_cap, axis=1), 1.0, 0.0
    ).astype(jnp.bfloat16)
    table_con = one_hot_table(edge_slots[0], replica_rows)
    table_var = one_hot_table(edge_slots[1], replica_rows)
    live_con = jnp.dot(table_con, slot_live[0], preferred_element_type=jnp.float32)
    live_var = jnp.dot(table_var, slot_live[1], preferred_element_type=jnp.float32)
    edge_active_mask = live_con * live_var
    edge_con = pick_rows(table_con, constraint_mirror_rows)
    edge_var = pick_rows(table_var, variable_mirror_rows)
    upstream_gradient = jnp.dot(
        table_var, cotangent_mirror_rows, preferred_element_type=jnp.float32
    )
    pre_act = (
        jnp.dot(edge_con, constraint_weight, preferred_element_type=jnp.float32)
        + jnp.dot(edge_var, variable_weight, preferred_element_type=jnp.float32)
        + bias[None, :]
    )
    sigmoid_pre = jax.nn.sigmoid(pre_act)
    message_derivative = sigmoid_pre * (1.0 + pre_act * (1.0 - sigmoid_pre))
    edge_delta = (upstream_gradient * message_derivative * edge_active_mask[:, None]).astype(
        jnp.bfloat16
    )
    sum_dims = (((0,), (0,)), ((), ()))
    constraint_projection_gradient = lax.dot_general(
        table_con, edge_delta, sum_dims, preferred_element_type=jnp.float32
    ).astype(jnp.bfloat16)
    variable_projection_gradient = lax.dot_general(
        table_var, edge_delta, sum_dims, preferred_element_type=jnp.float32
    ).astype(jnp.bfloat16)
    back_con = jnp.dot(
        constraint_projection_gradient, constraint_weight.T, preferred_element_type=jnp.float32
    ).astype(jnp.bfloat16)
    back_var = jnp.dot(
        variable_projection_gradient, variable_weight.T, preferred_element_type=jnp.float32
    ).astype(jnp.bfloat16)
    back_con = back_con.reshape(device_count, slot_cap, embedding_width)
    back_var = back_var.reshape(device_count, slot_cap, embedding_width)
    home_con, home_var = (
        lax.all_to_all(back_con, ("row", "col"), split_axis=0, concat_axis=0, tiled=True),
        lax.all_to_all(back_var, ("row", "col"), split_axis=0, concat_axis=0, tiled=True),
    )
    grad_con = lax.dot_general(
        select_con,
        home_con.reshape(replica_rows, embedding_width),
        sum_dims,
        preferred_element_type=jnp.float32,
    )
    grad_var = lax.dot_general(
        select_var,
        home_var.reshape(replica_rows, embedding_width),
        sum_dims,
        preferred_element_type=jnp.float32,
    )
    grad_var = variable_cotangent.astype(jnp.float32) + grad_var
    constraint_term = lax.dot_general(
        constraint_mirror_rows,
        constraint_projection_gradient,
        sum_dims,
        preferred_element_type=jnp.float32,
    )
    variable_term = lax.dot_general(
        variable_mirror_rows,
        variable_projection_gradient,
        sum_dims,
        preferred_element_type=jnp.float32,
    )
    term_bias = jnp.sum(edge_delta.astype(jnp.float32), axis=0)
    factor = float(device_count * edge_slots.shape[1]) ** (-0.5)
    bias_block = jnp.zeros((embedding_width, 128), jnp.float32).at[:, 0].set(term_bias)
    partials = jnp.concatenate([constraint_term, variable_term, bias_block], axis=1)
    share = embedding_width // device_count
    summed = lax.psum_scatter(partials.reshape(device_count, share, -1), ("row", "col"), scatter_dimension=0, tiled=True).reshape(share, -1)
    sum_con = summed[:, :embedding_width]
    sum_var = summed[:, embedding_width : 2 * embedding_width]
    sum_bias = summed[:, 2 * embedding_width]
    return (
        grad_con.astype(jnp.bfloat16),
        grad_var.astype(jnp.bfloat16),
        sum_con * factor,
        sum_var * factor,
        sum_bias * factor,
    )


def solution(mesh):
    placed = (
        P(("row", "col"), None),
        P(("row", "col"), None),
        P(("row", "col"), None),
        P(),
        P(),
        P(),
        P(None, ("row", "col"), None),
        P(None, ("row", "col"), None),
        P(None, ("row", "col")),
    )
    return jax.shard_map(
        on_device,
        mesh=mesh,
        in_specs=placed,
        out_specs=(
            P(("row", "col"), None),
            P(("row", "col"), None),
            P(("row", "col"), None),
            P(("row", "col"), None),
            P(("row", "col")),
        ),
        check_vma=False,
    )
```

```python
import jax
import jax.numpy as jnp
from jax import lax
from jax.sharding import PartitionSpec as P


def one_hot_table(indices, width):
    columns = lax.broadcasted_iota(jnp.int32, (indices.shape[0], width), 1)
    return jnp.where(columns == indices[:, None], 1.0, 0.0).astype(jnp.bfloat16)


def pick_rows(table, values):
    return jnp.dot(table, values, preferred_element_type=jnp.float32).astype(jnp.bfloat16)


def on_device(
    constraint_features,
    variable_features,
    variable_cotangent,
    constraint_weight,
    variable_weight,
    bias,
    send_rows,
    recv_count,
    edge_slots,
):
    device_count = lax.axis_size(("row", "col"))
    slot_cap = send_rows.shape[2] // device_count
    embedding_width = constraint_features.shape[1]
    replica_rows = device_count * slot_cap
    master_rows = constraint_features.shape[0]
    select_con = one_hot_table(send_rows[0, 0], master_rows)
    select_var = one_hot_table(send_rows[1, 0], master_rows)
    out_con = pick_rows(select_con, constraint_features).reshape(
        device_count, slot_cap, embedding_width
    )
    out_var = pick_rows(select_var, variable_features).reshape(
        device_count, slot_cap, embedding_width
    )
    out_cot = pick_rows(select_var, variable_cotangent).reshape(
        device_count, slot_cap, embedding_width
    )
    constraint_mirror_rows, variable_mirror_rows, cotangent_mirror_rows = (
        lax.all_to_all(out_con, ("row", "col"), split_axis=0, concat_axis=0, tiled=True),
        lax.all_to_all(out_var, ("row", "col"), split_axis=0, concat_axis=0, tiled=True),
        lax.all_to_all(out_cot, ("row", "col"), split_axis=0, concat_axis=0, tiled=True),
    )
    constraint_mirror_rows = constraint_mirror_rows.reshape(replica_rows, embedding_width)
    variable_mirror_rows = variable_mirror_rows.reshape(replica_rows, embedding_width)
    cotangent_mirror_rows = cotangent_mirror_rows.reshape(replica_rows, embedding_width)
    slot_pos = lax.broadcasted_iota(jnp.int32, (2, replica_rows), 1) % slot_cap
    slot_live = jnp.where(
        slot_pos < jnp.repeat(recv_count[:, 0], slot_cap, axis=1), 1.0, 0.0
    ).astype(jnp.bfloat16)
    table_con = one_hot_table(edge_slots[0], replica_rows)
    table_var = one_hot_table(edge_slots[1], replica_rows)
    live_con = jnp.dot(table_con, slot_live[0], preferred_element_type=jnp.float32)
    live_var = jnp.dot(table_var, slot_live[1], preferred_element_type=jnp.float32)
    edge_active_mask = live_con * live_var
    edge_con = pick_rows(table_con, constraint_mirror_rows)
    edge_var = pick_rows(table_var, variable_mirror_rows)
    upstream_gradient = jnp.dot(
        table_var, cotangent_mirror_rows, preferred_element_type=jnp.float32
    )
    pre_act = (
        jnp.dot(edge_con, constraint_weight, preferred_element_type=jnp.float32)
        + jnp.dot(edge_var, variable_weight, preferred_element_type=jnp.float32)
        + bias[None, :]
    )
    sigmoid_pre = jax.nn.sigmoid(pre_act)
    message_derivative = sigmoid_pre * (1.0 + pre_act * (1.0 - sigmoid_pre))
    edge_delta = (upstream_gradient * message_derivative * edge_active_mask[:, None]).astype(
        jnp.bfloat16
    )
    sum_dims = (((0,), (0,)), ((), ()))
    constraint_projection_gradient = lax.dot_general(
        table_con, edge_delta, sum_dims, preferred_element_type=jnp.float32
    ).astype(jnp.bfloat16)
    variable_projection_gradient = lax.dot_general(
        table_var, edge_delta, sum_dims, preferred_element_type=jnp.float32
    ).astype(jnp.bfloat16)
    back_con = jnp.dot(
        constraint_projection_gradient, constraint_weight.T, preferred_element_type=jnp.float32
    ).astype(jnp.bfloat16)
    back_var = jnp.dot(
        variable_projection_gradient, variable_weight.T, preferred_element_type=jnp.float32
    ).astype(jnp.bfloat16)
    back_con = back_con.reshape(device_count, slot_cap, embedding_width)
    back_var = back_var.reshape(device_count, slot_cap, embedding_width)
    home_con, home_var = (
        lax.all_to_all(back_con, ("row", "col"), split_axis=0, concat_axis=0, tiled=True),
        lax.all_to_all(back_var, ("row", "col"), split_axis=0, concat_axis=0, tiled=True),
    )
    grad_con = lax.dot_general(
        select_con,
        home_con.reshape(replica_rows, embedding_width),
        sum_dims,
        preferred_element_type=jnp.float32,
    )
    grad_var = lax.dot_general(
        select_var,
        home_var.reshape(replica_rows, embedding_width),
        sum_dims,
        preferred_element_type=jnp.float32,
    )
    grad_var = variable_cotangent.astype(jnp.float32) + grad_var
    constraint_term = lax.dot_general(
        constraint_mirror_rows,
        constraint_projection_gradient,
        sum_dims,
        preferred_element_type=jnp.float32,
    )
    variable_term = lax.dot_general(
        variable_mirror_rows,
        variable_projection_gradient,
        sum_dims,
        preferred_element_type=jnp.float32,
    )
    term_bias = jnp.sum(edge_delta.astype(jnp.float32), axis=0)
    factor = float(device_count * edge_slots.shape[1]) ** (-0.5)
    share = embedding_width // device_count
    lanes = 128
    bias_rows = jnp.zeros((device_count, 8, lanes), jnp.float32)
    bias_rows = bias_rows.at[:, 0, :share].set(term_bias.reshape(device_count, share))
    partials = jnp.concatenate(
        [
            constraint_term.reshape(device_count, -1, lanes),
            variable_term.reshape(device_count, -1, lanes),
            bias_rows,
        ],
        axis=1,
    )
    gathered = lax.all_to_all(partials, ("row", "col"), split_axis=0, concat_axis=0, tiled=True)
    summed = jnp.sum(gathered, axis=0)
    term_rows = share * embedding_width // lanes
    sum_con = summed[:term_rows].reshape(share, embedding_width)
    sum_var = summed[term_rows : 2 * term_rows].reshape(share, embedding_width)
    sum_bias = summed[2 * term_rows, :share]
    return (
        grad_con.astype(jnp.bfloat16),
        grad_var.astype(jnp.bfloat16),
        sum_con * factor,
        sum_var * factor,
        sum_bias * factor,
    )


def solution(mesh):
    placed = (
        P(("row", "col"), None),
        P(("row", "col"), None),
        P(("row", "col"), None),
        P(),
        P(),
        P(),
        P(None, ("row", "col"), None),
        P(None, ("row", "col"), None),
        P(None, ("row", "col")),
    )
    return jax.shard_map(
        on_device,
        mesh=mesh,
        in_specs=placed,
        out_specs=(
            P(("row", "col"), None),
            P(("row", "col"), None),
            P(("row", "col"), None),
            P(("row", "col"), None),
            P(("row", "col")),
        ),
        check_vma=False,
    )
```

```python
import jax
import jax.numpy as jnp
from jax import lax
from jax.sharding import Mesh, PartitionSpec as P

DEVICE_AXES = ("y", "c", "z", "x")


def one_hot_table(indices, width):
    columns = lax.broadcasted_iota(jnp.int32, (indices.shape[0], width), 1)
    return jnp.where(columns == indices[:, None], 1.0, 0.0).astype(jnp.bfloat16)


def pick_rows(table, values):
    return jnp.dot(table, values, preferred_element_type=jnp.float32).astype(jnp.bfloat16)


def on_device(
    constraint_features,
    variable_features,
    variable_cotangent,
    constraint_weight,
    variable_weight,
    bias,
    send_rows,
    recv_count,
    edge_slots,
):
    device_count = lax.axis_size(DEVICE_AXES)
    slot_cap = send_rows.shape[2] // device_count
    embedding_width = constraint_features.shape[1]
    replica_rows = device_count * slot_cap
    master_rows = constraint_features.shape[0]
    select_con = one_hot_table(send_rows[0, 0], master_rows)
    select_var = one_hot_table(send_rows[1, 0], master_rows)
    out_con = pick_rows(select_con, constraint_features).reshape(
        device_count, slot_cap, embedding_width
    )
    out_var = pick_rows(select_var, variable_features).reshape(
        device_count, slot_cap, embedding_width
    )
    out_cot = pick_rows(select_var, variable_cotangent).reshape(
        device_count, slot_cap, embedding_width
    )
    constraint_mirror_rows, variable_mirror_rows, cotangent_mirror_rows = (
        lax.all_to_all(out_con, DEVICE_AXES, split_axis=0, concat_axis=0, tiled=True),
        lax.all_to_all(out_var, DEVICE_AXES, split_axis=0, concat_axis=0, tiled=True),
        lax.all_to_all(out_cot, DEVICE_AXES, split_axis=0, concat_axis=0, tiled=True),
    )
    constraint_mirror_rows = constraint_mirror_rows.reshape(replica_rows, embedding_width)
    variable_mirror_rows = variable_mirror_rows.reshape(replica_rows, embedding_width)
    cotangent_mirror_rows = cotangent_mirror_rows.reshape(replica_rows, embedding_width)
    slot_pos = lax.broadcasted_iota(jnp.int32, (2, replica_rows), 1) % slot_cap
    slot_live = jnp.where(
        slot_pos < jnp.repeat(recv_count[:, 0], slot_cap, axis=1), 1.0, 0.0
    ).astype(jnp.bfloat16)
    table_con = one_hot_table(edge_slots[0], replica_rows)
    table_var = one_hot_table(edge_slots[1], replica_rows)
    live_con = jnp.dot(table_con, slot_live[0], preferred_element_type=jnp.float32)
    live_var = jnp.dot(table_var, slot_live[1], preferred_element_type=jnp.float32)
    edge_active_mask = live_con * live_var
    edge_con = pick_rows(table_con, constraint_mirror_rows)
    edge_var = pick_rows(table_var, variable_mirror_rows)
    upstream_gradient = jnp.dot(
        table_var, cotangent_mirror_rows, preferred_element_type=jnp.float32
    )
    pre_act = (
        jnp.dot(edge_con, constraint_weight, preferred_element_type=jnp.float32)
        + jnp.dot(edge_var, variable_weight, preferred_element_type=jnp.float32)
        + bias[None, :]
    )
    sigmoid_pre = jax.nn.sigmoid(pre_act)
    message_derivative = sigmoid_pre * (1.0 + pre_act * (1.0 - sigmoid_pre))
    edge_delta = (upstream_gradient * message_derivative * edge_active_mask[:, None]).astype(
        jnp.bfloat16
    )
    sum_dims = (((0,), (0,)), ((), ()))
    constraint_projection_gradient = lax.dot_general(
        table_con, edge_delta, sum_dims, preferred_element_type=jnp.float32
    ).astype(jnp.bfloat16)
    variable_projection_gradient = lax.dot_general(
        table_var, edge_delta, sum_dims, preferred_element_type=jnp.float32
    ).astype(jnp.bfloat16)
    back_con = jnp.dot(
        constraint_projection_gradient, constraint_weight.T, preferred_element_type=jnp.float32
    ).astype(jnp.bfloat16)
    back_var = jnp.dot(
        variable_projection_gradient, variable_weight.T, preferred_element_type=jnp.float32
    ).astype(jnp.bfloat16)
    back_con = back_con.reshape(device_count, slot_cap, embedding_width)
    back_var = back_var.reshape(device_count, slot_cap, embedding_width)
    home_con, home_var = (
        lax.all_to_all(back_con, DEVICE_AXES, split_axis=0, concat_axis=0, tiled=True),
        lax.all_to_all(back_var, DEVICE_AXES, split_axis=0, concat_axis=0, tiled=True),
    )
    grad_con = lax.dot_general(
        select_con,
        home_con.reshape(replica_rows, embedding_width),
        sum_dims,
        preferred_element_type=jnp.float32,
    )
    grad_var = lax.dot_general(
        select_var,
        home_var.reshape(replica_rows, embedding_width),
        sum_dims,
        preferred_element_type=jnp.float32,
    )
    grad_var = variable_cotangent.astype(jnp.float32) + grad_var
    constraint_term = lax.dot_general(
        constraint_mirror_rows,
        constraint_projection_gradient,
        sum_dims,
        preferred_element_type=jnp.float32,
    )
    variable_term = lax.dot_general(
        variable_mirror_rows,
        variable_projection_gradient,
        sum_dims,
        preferred_element_type=jnp.float32,
    )
    term_bias = jnp.sum(edge_delta.astype(jnp.float32), axis=0)
    factor = float(device_count * edge_slots.shape[1]) ** (-0.5)
    share = embedding_width // device_count
    lanes = 128
    bias_rows = jnp.zeros((device_count, 8, lanes), jnp.float32)
    bias_rows = bias_rows.at[:, 0, :share].set(term_bias.reshape(device_count, share))
    partials = jnp.concatenate(
        [
            constraint_term.reshape(device_count, -1, lanes),
            variable_term.reshape(device_count, -1, lanes),
            bias_rows,
        ],
        axis=1,
    )
    summed = partials.reshape(*(lax.axis_size(name) for name in DEVICE_AXES), -1, lanes)
    for axis_name, position in (("c", 1), ("x", 3), ("z", 2), ("y", 0)):
        sent = summed if axis_name == "c" else summed.astype(jnp.bfloat16)
        gathered = lax.all_to_all(sent, axis_name, position, position, tiled=True)
        summed = jnp.sum(gathered.astype(jnp.float32), axis=position, keepdims=True)
    summed = summed.reshape(-1, lanes)
    term_rows = share * embedding_width // lanes
    sum_con = summed[:term_rows].reshape(share, embedding_width)
    sum_var = summed[term_rows : 2 * term_rows].reshape(share, embedding_width)
    sum_bias = summed[2 * term_rows, :share]
    return (
        grad_con.astype(jnp.bfloat16),
        grad_var.astype(jnp.bfloat16),
        sum_con * factor,
        sum_var * factor,
        sum_bias * factor,
    )


def solution(mesh):
    placed = (
        P(DEVICE_AXES, None),
        P(DEVICE_AXES, None),
        P(DEVICE_AXES, None),
        P(),
        P(),
        P(),
        P(None, DEVICE_AXES, None),
        P(None, DEVICE_AXES, None),
        P(None, DEVICE_AXES),
    )
    rows, cols = mesh.devices.shape
    torus = Mesh(mesh.devices.reshape(rows // 2, 2, cols // 4, 4), DEVICE_AXES)
    return jax.shard_map(
        on_device,
        mesh=torus,
        in_specs=placed,
        out_specs=(
            P(DEVICE_AXES, None),
            P(DEVICE_AXES, None),
            P(DEVICE_AXES, None),
            P(DEVICE_AXES, None),
            P(DEVICE_AXES),
        ),
        check_vma=False,
    )
```

```python
import jax
import jax.numpy as jnp
from jax import lax
from jax.sharding import Mesh, PartitionSpec as P

DEVICE_AXES = ("y", "c", "z", "x")


def one_hot_table(indices, width):
    columns = lax.broadcasted_iota(jnp.int32, (indices.shape[0], width), 1)
    return jnp.where(columns == indices[:, None], 1.0, 0.0).astype(jnp.bfloat16)


def pick_rows(table, values):
    return jnp.dot(table, values, preferred_element_type=jnp.float32).astype(jnp.bfloat16)


def on_device(
    constraint_features,
    variable_features,
    variable_cotangent,
    constraint_weight,
    variable_weight,
    bias,
    send_rows,
    recv_count,
    edge_slots,
):
    device_count = lax.axis_size(DEVICE_AXES)
    slot_cap = send_rows.shape[2] // device_count
    embedding_width = constraint_features.shape[1]
    replica_rows = device_count * slot_cap
    master_rows = constraint_features.shape[0]
    select_con = one_hot_table(send_rows[0, 0], master_rows)
    select_var = one_hot_table(send_rows[1, 0], master_rows)
    out_con = pick_rows(select_con, constraint_features)
    out_var = pick_rows(select_var, variable_features)
    out_cot = pick_rows(select_var, variable_cotangent)
    outgoing = jnp.concatenate([out_con, out_var, out_cot], axis=1).reshape(
        device_count, slot_cap, 3 * embedding_width
    )
    incoming = lax.all_to_all(outgoing, DEVICE_AXES, split_axis=0, concat_axis=0, tiled=True)
    constraint_mirror_rows = incoming[:, :, :embedding_width]
    variable_mirror_rows = incoming[:, :, embedding_width : 2 * embedding_width]
    cotangent_mirror_rows = incoming[:, :, 2 * embedding_width :]
    constraint_mirror_rows = constraint_mirror_rows.reshape(replica_rows, embedding_width)
    variable_mirror_rows = variable_mirror_rows.reshape(replica_rows, embedding_width)
    cotangent_mirror_rows = cotangent_mirror_rows.reshape(replica_rows, embedding_width)
    slot_pos = lax.broadcasted_iota(jnp.int32, (2, replica_rows), 1) % slot_cap
    slot_live = jnp.where(
        slot_pos < jnp.repeat(recv_count[:, 0], slot_cap, axis=1), 1.0, 0.0
    ).astype(jnp.bfloat16)
    table_con = one_hot_table(edge_slots[0], replica_rows)
    table_var = one_hot_table(edge_slots[1], replica_rows)
    live_con = jnp.dot(table_con, slot_live[0], preferred_element_type=jnp.float32)
    live_var = jnp.dot(table_var, slot_live[1], preferred_element_type=jnp.float32)
    edge_active_mask = live_con * live_var
    edge_con = pick_rows(table_con, constraint_mirror_rows)
    edge_var = pick_rows(table_var, variable_mirror_rows)
    upstream_gradient = jnp.dot(
        table_var, cotangent_mirror_rows, preferred_element_type=jnp.float32
    )
    pre_act = (
        jnp.dot(edge_con, constraint_weight, preferred_element_type=jnp.float32)
        + jnp.dot(edge_var, variable_weight, preferred_element_type=jnp.float32)
        + bias[None, :]
    )
    sigmoid_pre = jax.nn.sigmoid(pre_act)
    message_derivative = sigmoid_pre * (1.0 + pre_act * (1.0 - sigmoid_pre))
    edge_delta = (upstream_gradient * message_derivative * edge_active_mask[:, None]).astype(
        jnp.bfloat16
    )
    sum_dims = (((0,), (0,)), ((), ()))
    constraint_projection_gradient = lax.dot_general(
        table_con, edge_delta, sum_dims, preferred_element_type=jnp.float32
    ).astype(jnp.bfloat16)
    variable_projection_gradient = lax.dot_general(
        table_var, edge_delta, sum_dims, preferred_element_type=jnp.float32
    ).astype(jnp.bfloat16)
    back_con = jnp.dot(
        constraint_projection_gradient, constraint_weight.T, preferred_element_type=jnp.float32
    ).astype(jnp.bfloat16)
    back_var = jnp.dot(
        variable_projection_gradient, variable_weight.T, preferred_element_type=jnp.float32
    ).astype(jnp.bfloat16)
    backward = jnp.concatenate([back_con, back_var], axis=1).reshape(
        device_count, slot_cap, 2 * embedding_width
    )
    homes = lax.all_to_all(backward, DEVICE_AXES, split_axis=0, concat_axis=0, tiled=True)
    home_con = homes[:, :, :embedding_width]
    home_var = homes[:, :, embedding_width:]
    grad_con = lax.dot_general(
        select_con,
        home_con.reshape(replica_rows, embedding_width),
        sum_dims,
        preferred_element_type=jnp.float32,
    )
    grad_var = lax.dot_general(
        select_var,
        home_var.reshape(replica_rows, embedding_width),
        sum_dims,
        preferred_element_type=jnp.float32,
    )
    grad_var = variable_cotangent.astype(jnp.float32) + grad_var
    constraint_term = lax.dot_general(
        constraint_mirror_rows,
        constraint_projection_gradient,
        sum_dims,
        preferred_element_type=jnp.float32,
    )
    variable_term = lax.dot_general(
        variable_mirror_rows,
        variable_projection_gradient,
        sum_dims,
        preferred_element_type=jnp.float32,
    )
    term_bias = jnp.sum(edge_delta.astype(jnp.float32), axis=0)
    factor = float(device_count * edge_slots.shape[1]) ** (-0.5)
    share = embedding_width // device_count
    lanes = 128
    bias_rows = jnp.zeros((device_count, 8, lanes), jnp.float32)
    bias_rows = bias_rows.at[:, 0, :share].set(term_bias.reshape(device_count, share))
    partials = jnp.concatenate(
        [
            constraint_term.reshape(device_count, -1, lanes),
            variable_term.reshape(device_count, -1, lanes),
            bias_rows,
        ],
        axis=1,
    )
    summed = partials.reshape(*(lax.axis_size(name) for name in DEVICE_AXES), -1, lanes)
    for axis_name, position in (("c", 1), ("x", 3), ("z", 2), ("y", 0)):
        sent = summed if axis_name == "c" else summed.astype(jnp.bfloat16)
        gathered = lax.all_to_all(sent, axis_name, position, position, tiled=True)
        summed = jnp.sum(gathered.astype(jnp.float32), axis=position, keepdims=True)
    summed = summed.reshape(-1, lanes)
    term_rows = share * embedding_width // lanes
    sum_con = summed[:term_rows].reshape(share, embedding_width)
    sum_var = summed[term_rows : 2 * term_rows].reshape(share, embedding_width)
    sum_bias = summed[2 * term_rows, :share]
    return (
        grad_con.astype(jnp.bfloat16),
        grad_var.astype(jnp.bfloat16),
        sum_con * factor,
        sum_var * factor,
        sum_bias * factor,
    )


def solution(mesh):
    placed = (
        P(DEVICE_AXES, None),
        P(DEVICE_AXES, None),
        P(DEVICE_AXES, None),
        P(),
        P(),
        P(),
        P(None, DEVICE_AXES, None),
        P(None, DEVICE_AXES, None),
        P(None, DEVICE_AXES),
    )
    rows, cols = mesh.devices.shape
    torus = Mesh(mesh.devices.reshape(rows // 2, 2, cols // 4, 4), DEVICE_AXES)
    return jax.shard_map(
        on_device,
        mesh=torus,
        in_specs=placed,
        out_specs=(
            P(DEVICE_AXES, None),
            P(DEVICE_AXES, None),
            P(DEVICE_AXES, None),
            P(DEVICE_AXES, None),
            P(DEVICE_AXES),
        ),
        check_vma=False,
    )
```

```python
import jax
import jax.numpy as jnp
from jax import lax
from jax.sharding import Mesh, PartitionSpec as P

DEVICE_AXES = ("y", "c", "z", "x")


def one_hot_table(indices, width):
    columns = lax.broadcasted_iota(jnp.int32, (indices.shape[0], width), 1)
    return jnp.where(columns == indices[:, None], 1.0, 0.0).astype(jnp.bfloat16)


def pick_rows(table, values):
    return jnp.dot(table, values, preferred_element_type=jnp.float32).astype(jnp.bfloat16)


def on_device(
    constraint_features,
    variable_features,
    variable_cotangent,
    constraint_weight,
    variable_weight,
    bias,
    send_rows,
    recv_count,
    edge_slots,
):
    device_count = lax.axis_size(DEVICE_AXES)
    slot_cap = send_rows.shape[2] // device_count
    embedding_width = constraint_features.shape[1]
    replica_rows = device_count * slot_cap
    master_rows = constraint_features.shape[0]
    select_con = one_hot_table(send_rows[0, 0], master_rows)
    select_var = one_hot_table(send_rows[1, 0], master_rows)
    out_con = pick_rows(select_con, constraint_features)
    out_var = pick_rows(select_var, variable_features)
    out_cot = pick_rows(select_var, variable_cotangent)
    slot_pos = lax.broadcasted_iota(jnp.int32, (2, replica_rows), 1) % slot_cap
    slot_live = jnp.where(
        slot_pos < jnp.repeat(recv_count[:, 0], slot_cap, axis=1), 1.0, 0.0
    ).astype(jnp.bfloat16)
    table_con = one_hot_table(edge_slots[0], replica_rows)
    table_var = one_hot_table(edge_slots[1], replica_rows)
    live_con = jnp.dot(table_con, slot_live[0], preferred_element_type=jnp.float32)
    live_var = jnp.dot(table_var, slot_live[1], preferred_element_type=jnp.float32)
    edge_active_mask = live_con * live_var
    half = embedding_width // 2
    mirrors = []
    pre_act = bias[None, :]
    upstream_parts = []
    for lo in (0, half):
        cols = slice(lo, lo + half)
        outgoing = jnp.concatenate(
            [out_con[:, cols], out_var[:, cols], out_cot[:, cols]], axis=1
        ).reshape(device_count, slot_cap, 3 * half)
        incoming = lax.all_to_all(outgoing, DEVICE_AXES, split_axis=0, concat_axis=0, tiled=True)
        incoming = incoming.reshape(replica_rows, 3 * half)
        con_part = incoming[:, :half]
        var_part = incoming[:, half : 2 * half]
        cot_part = incoming[:, 2 * half :]
        mirrors.append((con_part, var_part))
        edge_con = pick_rows(table_con, con_part)
        edge_var = pick_rows(table_var, var_part)
        upstream_parts.append(
            jnp.dot(table_var, cot_part, preferred_element_type=jnp.float32)
        )
        pre_act = (
            pre_act
            + jnp.dot(edge_con, constraint_weight[cols], preferred_element_type=jnp.float32)
            + jnp.dot(edge_var, variable_weight[cols], preferred_element_type=jnp.float32)
        )
    upstream_gradient = jnp.concatenate(upstream_parts, axis=1)
    sigmoid_pre = jax.nn.sigmoid(pre_act)
    message_derivative = sigmoid_pre * (1.0 + pre_act * (1.0 - sigmoid_pre))
    edge_delta = (upstream_gradient * message_derivative * edge_active_mask[:, None]).astype(
        jnp.bfloat16
    )
    sum_dims = (((0,), (0,)), ((), ()))
    constraint_projection_gradient = lax.dot_general(
        table_con, edge_delta, sum_dims, preferred_element_type=jnp.float32
    ).astype(jnp.bfloat16)
    variable_projection_gradient = lax.dot_general(
        table_var, edge_delta, sum_dims, preferred_element_type=jnp.float32
    ).astype(jnp.bfloat16)
    back_con = jnp.dot(
        constraint_projection_gradient, constraint_weight.T, preferred_element_type=jnp.float32
    ).astype(jnp.bfloat16)
    back_var = jnp.dot(
        variable_projection_gradient, variable_weight.T, preferred_element_type=jnp.float32
    ).astype(jnp.bfloat16)
    backward = jnp.concatenate([back_con, back_var], axis=1).reshape(
        device_count, slot_cap, 2 * embedding_width
    )
    homes = lax.all_to_all(backward, DEVICE_AXES, split_axis=0, concat_axis=0, tiled=True)
    home_con = homes[:, :, :embedding_width]
    home_var = homes[:, :, embedding_width:]
    grad_con = lax.dot_general(
        select_con,
        home_con.reshape(replica_rows, embedding_width),
        sum_dims,
        preferred_element_type=jnp.float32,
    )
    grad_var = lax.dot_general(
        select_var,
        home_var.reshape(replica_rows, embedding_width),
        sum_dims,
        preferred_element_type=jnp.float32,
    )
    grad_var = variable_cotangent.astype(jnp.float32) + grad_var
    constraint_term = jnp.concatenate(
        [
            lax.dot_general(
                con_part, constraint_projection_gradient, sum_dims,
                preferred_element_type=jnp.float32,
            )
            for con_part, _ in mirrors
        ],
        axis=0,
    )
    variable_term = jnp.concatenate(
        [
            lax.dot_general(
                var_part, variable_projection_gradient, sum_dims,
                preferred_element_type=jnp.float32,
            )
            for _, var_part in mirrors
        ],
        axis=0,
    )
    term_bias = jnp.sum(edge_delta.astype(jnp.float32), axis=0)
    factor = float(device_count * edge_slots.shape[1]) ** (-0.5)
    share = embedding_width // device_count
    lanes = 128
    bias_rows = jnp.zeros((device_count, 8, lanes), jnp.float32)
    bias_rows = bias_rows.at[:, 0, :share].set(term_bias.reshape(device_count, share))
    partials = jnp.concatenate(
        [
            constraint_term.reshape(device_count, -1, lanes),
            variable_term.reshape(device_count, -1, lanes),
            bias_rows,
        ],
        axis=1,
    )
    summed = partials.reshape(*(lax.axis_size(name) for name in DEVICE_AXES), -1, lanes)
    for axis_name, position in (("c", 1), ("x", 3), ("z", 2), ("y", 0)):
        sent = summed if axis_name == "c" else summed.astype(jnp.bfloat16)
        gathered = lax.all_to_all(sent, axis_name, position, position, tiled=True)
        summed = jnp.sum(gathered.astype(jnp.float32), axis=position, keepdims=True)
    summed = summed.reshape(-1, lanes)
    term_rows = share * embedding_width // lanes
    sum_con = summed[:term_rows].reshape(share, embedding_width)
    sum_var = summed[term_rows : 2 * term_rows].reshape(share, embedding_width)
    sum_bias = summed[2 * term_rows, :share]
    return (
        grad_con.astype(jnp.bfloat16),
        grad_var.astype(jnp.bfloat16),
        sum_con * factor,
        sum_var * factor,
        sum_bias * factor,
    )


def solution(mesh):
    placed = (
        P(DEVICE_AXES, None),
        P(DEVICE_AXES, None),
        P(DEVICE_AXES, None),
        P(),
        P(),
        P(),
        P(None, DEVICE_AXES, None),
        P(None, DEVICE_AXES, None),
        P(None, DEVICE_AXES),
    )
    rows, cols = mesh.devices.shape
    torus = Mesh(mesh.devices.reshape(rows // 2, 2, cols // 4, 4), DEVICE_AXES)
    return jax.shard_map(
        on_device,
        mesh=torus,
        in_specs=placed,
        out_specs=(
            P(DEVICE_AXES, None),
            P(DEVICE_AXES, None),
            P(DEVICE_AXES, None),
            P(DEVICE_AXES, None),
            P(DEVICE_AXES),
        ),
        check_vma=False,
    )
```

```python
import jax
import jax.numpy as jnp
from jax import lax
from jax.sharding import Mesh, PartitionSpec as P

DEVICE_AXES = ("y", "c", "z", "x")


def one_hot_table(indices, width):
    columns = lax.broadcasted_iota(jnp.int32, (indices.shape[0], width), 1)
    return jnp.where(columns == indices[:, None], 1.0, 0.0).astype(jnp.bfloat16)


def pick_rows(table, values):
    return jnp.dot(table, values, preferred_element_type=jnp.float32).astype(jnp.bfloat16)


def on_device(
    constraint_features,
    variable_features,
    variable_cotangent,
    constraint_weight,
    variable_weight,
    bias,
    send_rows,
    recv_count,
    edge_slots,
):
    device_count = lax.axis_size(DEVICE_AXES)
    slot_cap = send_rows.shape[2] // device_count
    embedding_width = constraint_features.shape[1]
    replica_rows = device_count * slot_cap
    master_rows = constraint_features.shape[0]
    select_con = one_hot_table(send_rows[0, 0], master_rows)
    select_var = one_hot_table(send_rows[1, 0], master_rows)
    out_con = pick_rows(select_con, constraint_features)
    out_var = pick_rows(select_var, variable_features)
    out_cot = pick_rows(select_var, variable_cotangent)
    outgoing = jnp.concatenate([out_con, out_var, out_cot], axis=1).reshape(
        device_count, slot_cap, 3 * embedding_width
    )
    incoming = lax.all_to_all(outgoing, DEVICE_AXES, split_axis=0, concat_axis=0, tiled=True)
    constraint_mirror_rows = incoming[:, :, :embedding_width]
    variable_mirror_rows = incoming[:, :, embedding_width : 2 * embedding_width]
    cotangent_mirror_rows = incoming[:, :, 2 * embedding_width :]
    constraint_mirror_rows = constraint_mirror_rows.reshape(replica_rows, embedding_width)
    variable_mirror_rows = variable_mirror_rows.reshape(replica_rows, embedding_width)
    cotangent_mirror_rows = cotangent_mirror_rows.reshape(replica_rows, embedding_width)
    slot_pos = lax.broadcasted_iota(jnp.int32, (2, replica_rows), 1) % slot_cap
    slot_live = jnp.where(
        slot_pos < jnp.repeat(recv_count[:, 0], slot_cap, axis=1), 1.0, 0.0
    ).astype(jnp.bfloat16)
    table_con = one_hot_table(edge_slots[0], replica_rows)
    table_var = one_hot_table(edge_slots[1], replica_rows)
    live_con = jnp.dot(table_con, slot_live[0], preferred_element_type=jnp.float32)
    live_var = jnp.dot(table_var, slot_live[1], preferred_element_type=jnp.float32)
    edge_active_mask = live_con * live_var
    edge_con = pick_rows(table_con, constraint_mirror_rows)
    edge_var = pick_rows(table_var, variable_mirror_rows)
    upstream_gradient = jnp.dot(
        table_var, cotangent_mirror_rows, preferred_element_type=jnp.float32
    )
    pre_act = (
        jnp.dot(edge_con, constraint_weight, preferred_element_type=jnp.float32)
        + jnp.dot(edge_var, variable_weight, preferred_element_type=jnp.float32)
        + bias[None, :]
    )
    sigmoid_pre = jax.nn.sigmoid(pre_act)
    message_derivative = sigmoid_pre * (1.0 + pre_act * (1.0 - sigmoid_pre))
    edge_delta = (upstream_gradient * message_derivative * edge_active_mask[:, None]).astype(
        jnp.bfloat16
    )
    sum_dims = (((0,), (0,)), ((), ()))
    constraint_projection_gradient = lax.dot_general(
        table_con, edge_delta, sum_dims, preferred_element_type=jnp.float32
    ).astype(jnp.bfloat16)
    variable_projection_gradient = lax.dot_general(
        table_var, edge_delta, sum_dims, preferred_element_type=jnp.float32
    ).astype(jnp.bfloat16)
    back_con = jnp.dot(
        constraint_projection_gradient, constraint_weight.T, preferred_element_type=jnp.float32
    ).astype(jnp.bfloat16)
    back_var = jnp.dot(
        variable_projection_gradient, variable_weight.T, preferred_element_type=jnp.float32
    ).astype(jnp.bfloat16)
    backward = jnp.concatenate([back_con, back_var], axis=1).reshape(
        device_count, slot_cap, 2 * embedding_width
    )
    homes = lax.all_to_all(backward, DEVICE_AXES, split_axis=0, concat_axis=0, tiled=True)
    home_con = homes[:, :, :embedding_width]
    home_var = homes[:, :, embedding_width:]
    grad_con = lax.dot_general(
        select_con,
        home_con.reshape(replica_rows, embedding_width),
        sum_dims,
        preferred_element_type=jnp.float32,
    )
    grad_var = lax.dot_general(
        select_var,
        home_var.reshape(replica_rows, embedding_width),
        sum_dims,
        preferred_element_type=jnp.float32,
    )
    grad_var = variable_cotangent.astype(jnp.float32) + grad_var
    constraint_term = lax.dot_general(
        constraint_mirror_rows,
        constraint_projection_gradient,
        sum_dims,
        preferred_element_type=jnp.float32,
    )
    variable_term = lax.dot_general(
        variable_mirror_rows,
        variable_projection_gradient,
        sum_dims,
        preferred_element_type=jnp.float32,
    )
    term_bias = jnp.sum(edge_delta.astype(jnp.float32), axis=0)
    factor = float(device_count * edge_slots.shape[1]) ** (-0.5)
    share = embedding_width // device_count
    lanes = 128
    bias_rows = jnp.zeros((device_count, 8, lanes), jnp.float32)
    bias_rows = bias_rows.at[:, 0, :share].set(term_bias.reshape(device_count, share))
    partials = jnp.concatenate(
        [
            constraint_term.reshape(device_count, -1, lanes),
            variable_term.reshape(device_count, -1, lanes),
            bias_rows,
        ],
        axis=1,
    )
    summed = partials.reshape(*(lax.axis_size(name) for name in DEVICE_AXES), -1, lanes)
    for axis_name, position in (("c", 1), ("x", 3), ("z", 2), ("y", 0)):
        ring = lax.axis_size(axis_name)
        me = lax.axis_index(axis_name)
        sent = summed if axis_name == "c" else summed.astype(jnp.bfloat16)
        total = lax.dynamic_slice_in_dim(summed, me, 1, position)
        for shift in range(1, ring):
            chunk = lax.dynamic_slice_in_dim(sent, (me + shift) % ring, 1, position)
            pairs = [(i, (i + shift) % ring) for i in range(ring)]
            total = total + lax.ppermute(chunk, axis_name, pairs).astype(jnp.float32)
        summed = total
    summed = summed.reshape(-1, lanes)
    term_rows = share * embedding_width // lanes
    sum_con = summed[:term_rows].reshape(share, embedding_width)
    sum_var = summed[term_rows : 2 * term_rows].reshape(share, embedding_width)
    sum_bias = summed[2 * term_rows, :share]
    return (
        grad_con.astype(jnp.bfloat16),
        grad_var.astype(jnp.bfloat16),
        sum_con * factor,
        sum_var * factor,
        sum_bias * factor,
    )


def solution(mesh):
    placed = (
        P(DEVICE_AXES, None),
        P(DEVICE_AXES, None),
        P(DEVICE_AXES, None),
        P(),
        P(),
        P(),
        P(None, DEVICE_AXES, None),
        P(None, DEVICE_AXES, None),
        P(None, DEVICE_AXES),
    )
    rows, cols = mesh.devices.shape
    torus = Mesh(mesh.devices.reshape(rows // 2, 2, cols // 4, 4), DEVICE_AXES)
    return jax.shard_map(
        on_device,
        mesh=torus,
        in_specs=placed,
        out_specs=(
            P(DEVICE_AXES, None),
            P(DEVICE_AXES, None),
            P(DEVICE_AXES, None),
            P(DEVICE_AXES, None),
            P(DEVICE_AXES),
        ),
        check_vma=False,
    )
```

```python
import jax
import jax.numpy as jnp
from jax import lax
from jax.sharding import Mesh, PartitionSpec as P

DEVICE_AXES = ("y", "c", "z", "x")


def one_hot_table(indices, width):
    columns = lax.broadcasted_iota(jnp.int32, (indices.shape[0], width), 1)
    return jnp.where(columns == indices[:, None], 1.0, 0.0).astype(jnp.bfloat16)


def pick_rows(table, values):
    return jnp.dot(table, values, preferred_element_type=jnp.float32).astype(jnp.bfloat16)


def on_device(
    constraint_features,
    variable_features,
    variable_cotangent,
    constraint_weight,
    variable_weight,
    bias,
    send_rows,
    recv_count,
    edge_slots,
):
    device_count = lax.axis_size(DEVICE_AXES)
    slot_cap = send_rows.shape[2] // device_count
    embedding_width = constraint_features.shape[1]
    replica_rows = device_count * slot_cap
    master_rows = constraint_features.shape[0]
    select_con = one_hot_table(send_rows[0, 0], master_rows)
    select_var = one_hot_table(send_rows[1, 0], master_rows)
    out_con = pick_rows(select_con, constraint_features)
    out_var = pick_rows(select_var, variable_features)
    out_cot = pick_rows(select_var, variable_cotangent)
    outgoing = jnp.concatenate([out_con, out_var, out_cot], axis=1).reshape(
        device_count, slot_cap, 3 * embedding_width
    )
    incoming = lax.all_to_all(outgoing, DEVICE_AXES, split_axis=0, concat_axis=0, tiled=True)
    constraint_mirror_rows = incoming[:, :, :embedding_width]
    variable_mirror_rows = incoming[:, :, embedding_width : 2 * embedding_width]
    cotangent_mirror_rows = incoming[:, :, 2 * embedding_width :]
    constraint_mirror_rows = constraint_mirror_rows.reshape(replica_rows, embedding_width)
    variable_mirror_rows = variable_mirror_rows.reshape(replica_rows, embedding_width)
    cotangent_mirror_rows = cotangent_mirror_rows.reshape(replica_rows, embedding_width)
    slot_pos = lax.broadcasted_iota(jnp.int32, (2, replica_rows), 1) % slot_cap
    slot_live = jnp.where(
        slot_pos < jnp.repeat(recv_count[:, 0], slot_cap, axis=1), 1.0, 0.0
    ).astype(jnp.bfloat16)
    table_con = one_hot_table(edge_slots[0], replica_rows)
    table_var = one_hot_table(edge_slots[1], replica_rows)
    live_con = jnp.dot(table_con, slot_live[0], preferred_element_type=jnp.float32)
    live_var = jnp.dot(table_var, slot_live[1], preferred_element_type=jnp.float32)
    edge_active_mask = live_con * live_var
    edge_con = pick_rows(table_con, constraint_mirror_rows)
    edge_var = pick_rows(table_var, variable_mirror_rows)
    upstream_gradient = jnp.dot(
        table_var, cotangent_mirror_rows, preferred_element_type=jnp.float32
    )
    pre_act = (
        jnp.dot(edge_con, constraint_weight, preferred_element_type=jnp.float32)
        + jnp.dot(edge_var, variable_weight, preferred_element_type=jnp.float32)
        + bias[None, :]
    )
    sigmoid_pre = jax.nn.sigmoid(pre_act)
    message_derivative = sigmoid_pre * (1.0 + pre_act * (1.0 - sigmoid_pre))
    edge_delta = (upstream_gradient * message_derivative * edge_active_mask[:, None]).astype(
        jnp.bfloat16
    )
    sum_dims = (((0,), (0,)), ((), ()))
    constraint_projection_gradient = lax.dot_general(
        table_con, edge_delta, sum_dims, preferred_element_type=jnp.float32
    ).astype(jnp.bfloat16)
    variable_projection_gradient = lax.dot_general(
        table_var, edge_delta, sum_dims, preferred_element_type=jnp.float32
    ).astype(jnp.bfloat16)
    back_con = jnp.dot(
        constraint_projection_gradient, constraint_weight.T, preferred_element_type=jnp.float32
    ).astype(jnp.bfloat16)
    back_var = jnp.dot(
        variable_projection_gradient, variable_weight.T, preferred_element_type=jnp.float32
    ).astype(jnp.bfloat16)
    backward = jnp.concatenate([back_con, back_var], axis=1).reshape(
        device_count, slot_cap, 2 * embedding_width
    )
    constraint_term = lax.dot_general(
        constraint_mirror_rows,
        constraint_projection_gradient,
        sum_dims,
        preferred_element_type=jnp.float32,
    )
    variable_term = lax.dot_general(
        variable_mirror_rows,
        variable_projection_gradient,
        sum_dims,
        preferred_element_type=jnp.float32,
    )
    term_bias = jnp.sum(edge_delta.astype(jnp.float32), axis=0)
    factor = float(device_count * edge_slots.shape[1]) ** (-0.5)
    share = embedding_width // device_count
    lanes = 128
    bias_rows = jnp.zeros((device_count, 8, lanes), jnp.float32)
    bias_rows = bias_rows.at[:, 0, :share].set(term_bias.reshape(device_count, share))
    partials = jnp.concatenate(
        [
            constraint_term.reshape(device_count, -1, lanes),
            variable_term.reshape(device_count, -1, lanes),
            bias_rows,
        ],
        axis=1,
    )
    summed = partials.reshape(*(lax.axis_size(name) for name in DEVICE_AXES), -1, lanes)
    for axis_name, position in (("c", 1), ("x", 3), ("z", 2), ("y", 0)):
        if axis_name == "x":
            backward, summed = lax.optimization_barrier((backward, summed))
            homes = lax.all_to_all(backward, DEVICE_AXES, split_axis=0, concat_axis=0, tiled=True)
            home_con = homes[:, :, :embedding_width]
            home_var = homes[:, :, embedding_width:]
        ring = lax.axis_size(axis_name)
        me = lax.axis_index(axis_name)
        sent = summed if axis_name == "c" else summed.astype(jnp.bfloat16)
        total = lax.dynamic_slice_in_dim(summed, me, 1, position)
        for shift in range(1, ring):
            chunk = lax.dynamic_slice_in_dim(sent, (me + shift) % ring, 1, position)
            pairs = [(i, (i + shift) % ring) for i in range(ring)]
            total = total + lax.ppermute(chunk, axis_name, pairs).astype(jnp.float32)
        summed = total
    summed = summed.reshape(-1, lanes)
    grad_con = lax.dot_general(
        select_con,
        home_con.reshape(replica_rows, embedding_width),
        sum_dims,
        preferred_element_type=jnp.float32,
    )
    grad_var = lax.dot_general(
        select_var,
        home_var.reshape(replica_rows, embedding_width),
        sum_dims,
        preferred_element_type=jnp.float32,
    )
    grad_var = variable_cotangent.astype(jnp.float32) + grad_var
    term_rows = share * embedding_width // lanes
    sum_con = summed[:term_rows].reshape(share, embedding_width)
    sum_var = summed[term_rows : 2 * term_rows].reshape(share, embedding_width)
    sum_bias = summed[2 * term_rows, :share]
    return (
        grad_con.astype(jnp.bfloat16),
        grad_var.astype(jnp.bfloat16),
        sum_con * factor,
        sum_var * factor,
        sum_bias * factor,
    )


def solution(mesh):
    placed = (
        P(DEVICE_AXES, None),
        P(DEVICE_AXES, None),
        P(DEVICE_AXES, None),
        P(),
        P(),
        P(),
        P(None, DEVICE_AXES, None),
        P(None, DEVICE_AXES, None),
        P(None, DEVICE_AXES),
    )
    rows, cols = mesh.devices.shape
    torus = Mesh(mesh.devices.reshape(rows // 2, 2, cols // 4, 4), DEVICE_AXES)
    return jax.shard_map(
        on_device,
        mesh=torus,
        in_specs=placed,
        out_specs=(
            P(DEVICE_AXES, None),
            P(DEVICE_AXES, None),
            P(DEVICE_AXES, None),
            P(DEVICE_AXES, None),
            P(DEVICE_AXES),
        ),
        check_vma=False,
    )
```

```python
import jax
import jax.numpy as jnp
from jax import lax
from jax.sharding import Mesh, PartitionSpec as P

DEVICE_AXES = ("y", "c", "z", "x")


def one_hot_table(indices, width):
    columns = lax.broadcasted_iota(jnp.int32, (indices.shape[0], width), 1)
    return jnp.where(columns == indices[:, None], 1.0, 0.0).astype(jnp.bfloat16)


def pick_rows(table, values):
    return jnp.dot(table, values, preferred_element_type=jnp.float32).astype(jnp.bfloat16)


def on_device(
    constraint_features,
    variable_features,
    variable_cotangent,
    constraint_weight,
    variable_weight,
    bias,
    send_rows,
    recv_count,
    edge_slots,
):
    device_count = lax.axis_size(DEVICE_AXES)
    slot_cap = send_rows.shape[2] // device_count
    embedding_width = constraint_features.shape[1]
    replica_rows = device_count * slot_cap
    master_rows = constraint_features.shape[0]
    select_con = one_hot_table(send_rows[0, 0], master_rows)
    select_var = one_hot_table(send_rows[1, 0], master_rows)
    out_con = pick_rows(select_con, constraint_features)
    out_var = pick_rows(select_var, variable_features)
    out_cot = pick_rows(select_var, variable_cotangent)
    outgoing = jnp.concatenate([out_con, out_var, out_cot], axis=1).reshape(
        device_count, slot_cap, 3 * embedding_width
    )
    incoming = lax.all_to_all(outgoing, DEVICE_AXES, split_axis=0, concat_axis=0, tiled=True)
    constraint_mirror_rows = incoming[:, :, :embedding_width]
    variable_mirror_rows = incoming[:, :, embedding_width : 2 * embedding_width]
    cotangent_mirror_rows = incoming[:, :, 2 * embedding_width :]
    slot_pos = lax.broadcasted_iota(jnp.int32, (2, replica_rows), 1) % slot_cap
    slot_live = jnp.where(
        slot_pos < jnp.repeat(recv_count[:, 0], slot_cap, axis=1), 1.0, 0.0
    ).astype(jnp.bfloat16)
    table_con = one_hot_table(edge_slots[0], replica_rows)
    table_var = one_hot_table(edge_slots[1], replica_rows)
    live_con = jnp.dot(table_con, slot_live[0], preferred_element_type=jnp.float32)
    live_var = jnp.dot(table_var, slot_live[1], preferred_element_type=jnp.float32)
    edge_active_mask = live_con * live_var
    slot_dims = (((1, 2), (0, 1)), ((), ()))
    table_con3 = table_con.reshape(-1, device_count, slot_cap)
    table_var3 = table_var.reshape(-1, device_count, slot_cap)
    edge_con = lax.dot_general(
        table_con3, constraint_mirror_rows, slot_dims, preferred_element_type=jnp.float32
    ).astype(jnp.bfloat16)
    edge_var = lax.dot_general(
        table_var3, variable_mirror_rows, slot_dims, preferred_element_type=jnp.float32
    ).astype(jnp.bfloat16)
    upstream_gradient = lax.dot_general(
        table_var3, cotangent_mirror_rows, slot_dims, preferred_element_type=jnp.float32
    )
    pre_act = (
        jnp.dot(edge_con, constraint_weight, preferred_element_type=jnp.float32)
        + jnp.dot(edge_var, variable_weight, preferred_element_type=jnp.float32)
        + bias[None, :]
    )
    sigmoid_pre = jax.nn.sigmoid(pre_act)
    message_derivative = sigmoid_pre * (1.0 + pre_act * (1.0 - sigmoid_pre))
    edge_delta = (upstream_gradient * message_derivative * edge_active_mask[:, None]).astype(
        jnp.bfloat16
    )
    sum_dims = (((0,), (0,)), ((), ()))
    constraint_projection_gradient = lax.dot_general(
        table_con, edge_delta, sum_dims, preferred_element_type=jnp.float32
    ).astype(jnp.bfloat16)
    variable_projection_gradient = lax.dot_general(
        table_var, edge_delta, sum_dims, preferred_element_type=jnp.float32
    ).astype(jnp.bfloat16)
    back_con = jnp.dot(
        constraint_projection_gradient, constraint_weight.T, preferred_element_type=jnp.float32
    ).astype(jnp.bfloat16)
    back_var = jnp.dot(
        variable_projection_gradient, variable_weight.T, preferred_element_type=jnp.float32
    ).astype(jnp.bfloat16)
    backward = jnp.concatenate([back_con, back_var], axis=1).reshape(
        device_count, slot_cap, 2 * embedding_width
    )
    constraint_term = lax.dot_general(
        constraint_mirror_rows,
        constraint_projection_gradient.reshape(device_count, slot_cap, embedding_width),
        (((0, 1), (0, 1)), ((), ())),
        preferred_element_type=jnp.float32,
    )
    variable_term = lax.dot_general(
        variable_mirror_rows,
        variable_projection_gradient.reshape(device_count, slot_cap, embedding_width),
        (((0, 1), (0, 1)), ((), ())),
        preferred_element_type=jnp.float32,
    )
    term_bias = jnp.sum(edge_delta.astype(jnp.float32), axis=0)
    factor = float(device_count * edge_slots.shape[1]) ** (-0.5)
    share = embedding_width // device_count
    lanes = 128
    bias_rows = jnp.zeros((device_count, 8, lanes), jnp.float32)
    bias_rows = bias_rows.at[:, 0, :share].set(term_bias.reshape(device_count, share))
    partials = jnp.concatenate(
        [
            constraint_term.reshape(device_count, -1, lanes),
            variable_term.reshape(device_count, -1, lanes),
            bias_rows,
        ],
        axis=1,
    )
    summed = partials.reshape(*(lax.axis_size(name) for name in DEVICE_AXES), -1, lanes)
    for axis_name, position in (("c", 1), ("x", 3), ("z", 2), ("y", 0)):
        if axis_name == "x":
            backward, summed = lax.optimization_barrier((backward, summed))
            homes = lax.all_to_all(backward, DEVICE_AXES, split_axis=0, concat_axis=0, tiled=True)
            home_con = homes[:, :, :embedding_width]
            home_var = homes[:, :, embedding_width:]
        ring = lax.axis_size(axis_name)
        me = lax.axis_index(axis_name)
        sent = summed if axis_name == "c" else summed.astype(jnp.bfloat16)
        total = lax.dynamic_slice_in_dim(summed, me, 1, position)
        for shift in range(1, ring):
            chunk = lax.dynamic_slice_in_dim(sent, (me + shift) % ring, 1, position)
            pairs = [(i, (i + shift) % ring) for i in range(ring)]
            total = total + lax.ppermute(chunk, axis_name, pairs).astype(jnp.float32)
        summed = total
    summed = summed.reshape(-1, lanes)
    grad_con = lax.dot_general(
        select_con.reshape(device_count, slot_cap, -1),
        home_con,
        (((0, 1), (0, 1)), ((), ())),
        preferred_element_type=jnp.float32,
    )
    grad_var = lax.dot_general(
        select_var.reshape(device_count, slot_cap, -1),
        home_var,
        (((0, 1), (0, 1)), ((), ())),
        preferred_element_type=jnp.float32,
    )
    grad_var = variable_cotangent.astype(jnp.float32) + grad_var
    term_rows = share * embedding_width // lanes
    sum_con = summed[:term_rows].reshape(share, embedding_width)
    sum_var = summed[term_rows : 2 * term_rows].reshape(share, embedding_width)
    sum_bias = summed[2 * term_rows, :share]
    return (
        grad_con.astype(jnp.bfloat16),
        grad_var.astype(jnp.bfloat16),
        sum_con * factor,
        sum_var * factor,
        sum_bias * factor,
    )


def solution(mesh):
    placed = (
        P(DEVICE_AXES, None),
        P(DEVICE_AXES, None),
        P(DEVICE_AXES, None),
        P(),
        P(),
        P(),
        P(None, DEVICE_AXES, None),
        P(None, DEVICE_AXES, None),
        P(None, DEVICE_AXES),
    )
    rows, cols = mesh.devices.shape
    torus = Mesh(mesh.devices.reshape(rows // 2, 2, cols // 4, 4), DEVICE_AXES)
    return jax.shard_map(
        on_device,
        mesh=torus,
        in_specs=placed,
        out_specs=(
            P(DEVICE_AXES, None),
            P(DEVICE_AXES, None),
            P(DEVICE_AXES, None),
            P(DEVICE_AXES, None),
            P(DEVICE_AXES),
        ),
        check_vma=False,
    )
```

```python
import jax
import jax.numpy as jnp
from jax import lax
from jax.sharding import Mesh, PartitionSpec as P

DEVICE_AXES = ("y", "c", "z", "x")


def one_hot_table(indices, width):
    columns = lax.broadcasted_iota(jnp.int32, (indices.shape[0], width), 1)
    return jnp.where(columns == indices[:, None], 1.0, 0.0).astype(jnp.bfloat16)


def pick_rows(table, values):
    return jnp.dot(table, values, preferred_element_type=jnp.float32).astype(jnp.bfloat16)


def on_device(
    constraint_features,
    variable_features,
    variable_cotangent,
    constraint_weight,
    variable_weight,
    bias,
    send_rows,
    recv_count,
    edge_slots,
):
    device_count = lax.axis_size(DEVICE_AXES)
    slot_cap = send_rows.shape[2] // device_count
    embedding_width = constraint_features.shape[1]
    replica_rows = device_count * slot_cap
    master_rows = constraint_features.shape[0]
    select_con = one_hot_table(send_rows[0, 0], master_rows)
    select_var = one_hot_table(send_rows[1, 0], master_rows)
    rows_con = send_rows[0, 0]
    rows_var = send_rows[1, 0]
    outgoing = jnp.concatenate(
        [
            jnp.take(constraint_features, rows_con, axis=0, mode="clip"),
            jnp.take(variable_features, rows_var, axis=0, mode="clip"),
            jnp.take(variable_cotangent, rows_var, axis=0, mode="clip"),
        ],
        axis=1,
    ).reshape(
        device_count, slot_cap, 3 * embedding_width
    )
    incoming = lax.all_to_all(outgoing, DEVICE_AXES, split_axis=0, concat_axis=0, tiled=True)
    constraint_mirror_rows = incoming[:, :, :embedding_width]
    variable_mirror_rows = incoming[:, :, embedding_width : 2 * embedding_width]
    cotangent_mirror_rows = incoming[:, :, 2 * embedding_width :]
    slot_pos = lax.broadcasted_iota(jnp.int32, (2, replica_rows), 1) % slot_cap
    slot_live = jnp.where(
        slot_pos < jnp.repeat(recv_count[:, 0], slot_cap, axis=1), 1.0, 0.0
    ).astype(jnp.bfloat16)
    table_con = one_hot_table(edge_slots[0], replica_rows)
    table_var = one_hot_table(edge_slots[1], replica_rows)
    live_con = jnp.dot(table_con, slot_live[0], preferred_element_type=jnp.float32)
    live_var = jnp.dot(table_var, slot_live[1], preferred_element_type=jnp.float32)
    edge_active_mask = live_con * live_var
    slot_dims = (((1, 2), (0, 1)), ((), ()))
    table_con3 = table_con.reshape(-1, device_count, slot_cap)
    table_var3 = table_var.reshape(-1, device_count, slot_cap)
    edge_con = lax.dot_general(
        table_con3, constraint_mirror_rows, slot_dims, preferred_element_type=jnp.float32
    ).astype(jnp.bfloat16)
    edge_var = lax.dot_general(
        table_var3, variable_mirror_rows, slot_dims, preferred_element_type=jnp.float32
    ).astype(jnp.bfloat16)
    upstream_gradient = lax.dot_general(
        table_var3, cotangent_mirror_rows, slot_dims, preferred_element_type=jnp.float32
    )
    pre_act = (
        jnp.dot(edge_con, constraint_weight, preferred_element_type=jnp.float32)
        + jnp.dot(edge_var, variable_weight, preferred_element_type=jnp.float32)
        + bias[None, :]
    )
    sigmoid_pre = jax.nn.sigmoid(pre_act)
    message_derivative = sigmoid_pre * (1.0 + pre_act * (1.0 - sigmoid_pre))
    edge_delta = (upstream_gradient * message_derivative * edge_active_mask[:, None]).astype(
        jnp.bfloat16
    )
    sum_dims = (((0,), (0,)), ((), ()))
    constraint_projection_gradient = lax.dot_general(
        table_con, edge_delta, sum_dims, preferred_element_type=jnp.float32
    ).astype(jnp.bfloat16)
    variable_projection_gradient = lax.dot_general(
        table_var, edge_delta, sum_dims, preferred_element_type=jnp.float32
    ).astype(jnp.bfloat16)
    back_con = jnp.dot(
        constraint_projection_gradient, constraint_weight.T, preferred_element_type=jnp.float32
    ).astype(jnp.bfloat16)
    back_var = jnp.dot(
        variable_projection_gradient, variable_weight.T, preferred_element_type=jnp.float32
    ).astype(jnp.bfloat16)
    backward = jnp.concatenate([back_con, back_var], axis=1).reshape(
        device_count, slot_cap, 2 * embedding_width
    )
    constraint_term = lax.dot_general(
        constraint_mirror_rows,
        constraint_projection_gradient.reshape(device_count, slot_cap, embedding_width),
        (((0, 1), (0, 1)), ((), ())),
        preferred_element_type=jnp.float32,
    )
    variable_term = lax.dot_general(
        variable_mirror_rows,
        variable_projection_gradient.reshape(device_count, slot_cap, embedding_width),
        (((0, 1), (0, 1)), ((), ())),
        preferred_element_type=jnp.float32,
    )
    term_bias = jnp.sum(edge_delta.astype(jnp.float32), axis=0)
    factor = float(device_count * edge_slots.shape[1]) ** (-0.5)
    share = embedding_width // device_count
    lanes = 128
    bias_rows = jnp.zeros((device_count, 8, lanes), jnp.float32)
    bias_rows = bias_rows.at[:, 0, :share].set(term_bias.reshape(device_count, share))
    partials = jnp.concatenate(
        [
            constraint_term.reshape(device_count, -1, lanes),
            variable_term.reshape(device_count, -1, lanes),
            bias_rows,
        ],
        axis=1,
    )
    summed = partials.reshape(*(lax.axis_size(name) for name in DEVICE_AXES), -1, lanes)
    for axis_name, position in (("c", 1), ("x", 3), ("z", 2), ("y", 0)):
        if axis_name == "x":
            backward, summed = lax.optimization_barrier((backward, summed))
            homes = lax.all_to_all(backward, DEVICE_AXES, split_axis=0, concat_axis=0, tiled=True)
            home_con = homes[:, :, :embedding_width]
            home_var = homes[:, :, embedding_width:]
        ring = lax.axis_size(axis_name)
        me = lax.axis_index(axis_name)
        sent = summed if axis_name == "c" else summed.astype(jnp.bfloat16)
        total = lax.dynamic_slice_in_dim(summed, me, 1, position)
        for shift in range(1, ring):
            chunk = lax.dynamic_slice_in_dim(sent, (me + shift) % ring, 1, position)
            pairs = [(i, (i + shift) % ring) for i in range(ring)]
            total = total + lax.ppermute(chunk, axis_name, pairs).astype(jnp.float32)
        summed = total
    summed = summed.reshape(-1, lanes)
    grad_con = lax.dot_general(
        select_con.reshape(device_count, slot_cap, -1),
        home_con,
        (((0, 1), (0, 1)), ((), ())),
        preferred_element_type=jnp.float32,
    )
    grad_var = lax.dot_general(
        select_var.reshape(device_count, slot_cap, -1),
        home_var,
        (((0, 1), (0, 1)), ((), ())),
        preferred_element_type=jnp.float32,
    )
    grad_var = variable_cotangent.astype(jnp.float32) + grad_var
    term_rows = share * embedding_width // lanes
    sum_con = summed[:term_rows].reshape(share, embedding_width)
    sum_var = summed[term_rows : 2 * term_rows].reshape(share, embedding_width)
    sum_bias = summed[2 * term_rows, :share]
    return (
        grad_con.astype(jnp.bfloat16),
        grad_var.astype(jnp.bfloat16),
        sum_con * factor,
        sum_var * factor,
        sum_bias * factor,
    )


def solution(mesh):
    placed = (
        P(DEVICE_AXES, None),
        P(DEVICE_AXES, None),
        P(DEVICE_AXES, None),
        P(),
        P(),
        P(),
        P(None, DEVICE_AXES, None),
        P(None, DEVICE_AXES, None),
        P(None, DEVICE_AXES),
    )
    rows, cols = mesh.devices.shape
    torus = Mesh(mesh.devices.reshape(rows // 2, 2, cols // 4, 4), DEVICE_AXES)
    return jax.shard_map(
        on_device,
        mesh=torus,
        in_specs=placed,
        out_specs=(
            P(DEVICE_AXES, None),
            P(DEVICE_AXES, None),
            P(DEVICE_AXES, None),
            P(DEVICE_AXES, None),
            P(DEVICE_AXES),
        ),
        check_vma=False,
    )
```

```python
import jax
import jax.numpy as jnp
from jax import lax
from jax.sharding import Mesh, PartitionSpec as P

DEVICE_AXES = ("y", "c", "z", "x")


def one_hot_table(indices, width):
    columns = lax.broadcasted_iota(jnp.int32, (indices.shape[0], width), 1)
    return jnp.where(columns == indices[:, None], 1.0, 0.0).astype(jnp.bfloat16)


def pick_rows(table, values):
    return jnp.dot(table, values, preferred_element_type=jnp.float32).astype(jnp.bfloat16)


def on_device(
    constraint_features,
    variable_features,
    variable_cotangent,
    constraint_weight,
    variable_weight,
    bias,
    send_rows,
    recv_count,
    edge_slots,
):
    device_count = lax.axis_size(DEVICE_AXES)
    slot_cap = send_rows.shape[2] // device_count
    embedding_width = constraint_features.shape[1]
    replica_rows = device_count * slot_cap
    master_rows = constraint_features.shape[0]
    select_con = one_hot_table(send_rows[0, 0], master_rows)
    select_var = one_hot_table(send_rows[1, 0], master_rows)
    out_con = pick_rows(select_con, constraint_features)
    out_var = pick_rows(select_var, variable_features)
    out_cot = pick_rows(select_var, variable_cotangent)
    outgoing = jnp.concatenate([out_con, out_var, out_cot], axis=1).reshape(
        device_count, slot_cap, 3 * embedding_width
    )
    incoming = lax.all_to_all(outgoing, DEVICE_AXES, split_axis=0, concat_axis=0, tiled=True)
    constraint_mirror_rows = incoming[:, :, :embedding_width]
    variable_mirror_rows = incoming[:, :, embedding_width : 2 * embedding_width]
    cotangent_mirror_rows = incoming[:, :, 2 * embedding_width :]
    slot_pos = lax.broadcasted_iota(jnp.int32, (2, replica_rows), 1) % slot_cap
    slot_live = jnp.where(
        slot_pos < jnp.repeat(recv_count[:, 0], slot_cap, axis=1), 1.0, 0.0
    ).astype(jnp.bfloat16)
    table_con = one_hot_table(edge_slots[0], replica_rows)
    table_var = one_hot_table(edge_slots[1], replica_rows)
    live_con = jnp.dot(table_con, slot_live[0], preferred_element_type=jnp.float32)
    live_var = jnp.dot(table_var, slot_live[1], preferred_element_type=jnp.float32)
    edge_active_mask = live_con * live_var
    slot_dims = (((1, 2), (0, 1)), ((), ()))
    table_con3 = table_con.reshape(-1, device_count, slot_cap)
    table_var3 = table_var.reshape(-1, device_count, slot_cap)
    edge_con = lax.dot_general(
        table_con3, constraint_mirror_rows, slot_dims, preferred_element_type=jnp.float32
    ).astype(jnp.bfloat16)
    edge_var = lax.dot_general(
        table_var3, variable_mirror_rows, slot_dims, preferred_element_type=jnp.float32
    ).astype(jnp.bfloat16)
    upstream_gradient = lax.dot_general(
        table_var3, cotangent_mirror_rows, slot_dims, preferred_element_type=jnp.float32
    )
    pre_act = (
        jnp.dot(edge_con, constraint_weight, preferred_element_type=jnp.float32)
        + jnp.dot(edge_var, variable_weight, preferred_element_type=jnp.float32)
        + bias[None, :]
    )
    sigmoid_pre = jax.nn.sigmoid(pre_act)
    message_derivative = sigmoid_pre * (1.0 + pre_act * (1.0 - sigmoid_pre))
    edge_delta = (upstream_gradient * message_derivative * edge_active_mask[:, None]).astype(
        jnp.bfloat16
    )
    sum_dims = (((0,), (0,)), ((), ()))
    constraint_projection_gradient = lax.dot_general(
        table_con, edge_delta, sum_dims, preferred_element_type=jnp.float32
    ).astype(jnp.bfloat16)
    variable_projection_gradient = lax.dot_general(
        table_var, edge_delta, sum_dims, preferred_element_type=jnp.float32
    ).astype(jnp.bfloat16)
    back_con = jnp.dot(
        constraint_projection_gradient, constraint_weight.T, preferred_element_type=jnp.float32
    ).astype(jnp.bfloat16)
    back_var = jnp.dot(
        variable_projection_gradient, variable_weight.T, preferred_element_type=jnp.float32
    ).astype(jnp.bfloat16)
    backward = jnp.concatenate([back_con, back_var], axis=1).reshape(
        device_count, slot_cap, 2 * embedding_width
    )
    constraint_term = lax.dot_general(
        constraint_mirror_rows,
        constraint_projection_gradient.reshape(device_count, slot_cap, embedding_width),
        (((0, 1), (0, 1)), ((), ())),
        preferred_element_type=jnp.float32,
    )
    variable_term = lax.dot_general(
        variable_mirror_rows,
        variable_projection_gradient.reshape(device_count, slot_cap, embedding_width),
        (((0, 1), (0, 1)), ((), ())),
        preferred_element_type=jnp.float32,
    )
    term_bias = jnp.sum(edge_delta.astype(jnp.float32), axis=0)
    factor = float(device_count * edge_slots.shape[1]) ** (-0.5)
    share = embedding_width // device_count
    lanes = 128
    bias_rows = jnp.zeros((device_count, 8, lanes), jnp.float32)
    bias_rows = bias_rows.at[:, 0, :share].set(term_bias.reshape(device_count, share))
    partials = jnp.concatenate(
        [
            constraint_term.reshape(device_count, -1, lanes),
            variable_term.reshape(device_count, -1, lanes),
            bias_rows,
        ],
        axis=1,
    )
    grid = partials.reshape(*(lax.axis_size(name) for name in DEVICE_AXES), -1, lanes)
    pieces = [grid[..., :40, :], grid[..., 40:, :]]
    for axis_name, position in (("c", 1), ("x", 3), ("z", 2), ("y", 0)):
        if axis_name == "x":
            backward, pieces = lax.optimization_barrier((backward, pieces))
            homes = lax.all_to_all(backward, DEVICE_AXES, split_axis=0, concat_axis=0, tiled=True)
            home_con = homes[:, :, :embedding_width]
            home_var = homes[:, :, embedding_width:]
        ring = lax.axis_size(axis_name)
        me = lax.axis_index(axis_name)
        reduced = []
        for piece in pieces:
            sent = piece if axis_name == "c" else piece.astype(jnp.bfloat16)
            total = lax.dynamic_slice_in_dim(piece, me, 1, position)
            for shift in range(1, ring):
                chunk = lax.dynamic_slice_in_dim(sent, (me + shift) % ring, 1, position)
                pairs = [(i, (i + shift) % ring) for i in range(ring)]
                total = total + lax.ppermute(chunk, axis_name, pairs).astype(jnp.float32)
            reduced.append(total)
        pieces = reduced
    summed = jnp.concatenate(pieces, axis=-2)
    summed = summed.reshape(-1, lanes)
    grad_con = lax.dot_general(
        select_con.reshape(device_count, slot_cap, -1),
        home_con,
        (((0, 1), (0, 1)), ((), ())),
        preferred_element_type=jnp.float32,
    )
    grad_var = lax.dot_general(
        select_var.reshape(device_count, slot_cap, -1),
        home_var,
        (((0, 1), (0, 1)), ((), ())),
        preferred_element_type=jnp.float32,
    )
    grad_var = variable_cotangent.astype(jnp.float32) + grad_var
    term_rows = share * embedding_width // lanes
    sum_con = summed[:term_rows].reshape(share, embedding_width)
    sum_var = summed[term_rows : 2 * term_rows].reshape(share, embedding_width)
    sum_bias = summed[2 * term_rows, :share]
    return (
        grad_con.astype(jnp.bfloat16),
        grad_var.astype(jnp.bfloat16),
        sum_con * factor,
        sum_var * factor,
        sum_bias * factor,
    )


def solution(mesh):
    placed = (
        P(DEVICE_AXES, None),
        P(DEVICE_AXES, None),
        P(DEVICE_AXES, None),
        P(),
        P(),
        P(),
        P(None, DEVICE_AXES, None),
        P(None, DEVICE_AXES, None),
        P(None, DEVICE_AXES),
    )
    rows, cols = mesh.devices.shape
    torus = Mesh(mesh.devices.reshape(rows // 2, 2, cols // 4, 4), DEVICE_AXES)
    return jax.shard_map(
        on_device,
        mesh=torus,
        in_specs=placed,
        out_specs=(
            P(DEVICE_AXES, None),
            P(DEVICE_AXES, None),
            P(DEVICE_AXES, None),
            P(DEVICE_AXES, None),
            P(DEVICE_AXES),
        ),
        check_vma=False,
    )
```

```python
import jax
import jax.numpy as jnp
from jax import lax
from jax.sharding import Mesh, PartitionSpec as P

DEVICE_AXES = ("y", "c", "z", "x")


def one_hot_table(indices, width):
    columns = lax.broadcasted_iota(jnp.int32, (indices.shape[0], width), 1)
    return jnp.where(columns == indices[:, None], 1.0, 0.0).astype(jnp.bfloat16)


def pick_rows(table, values):
    return jnp.dot(table, values, preferred_element_type=jnp.float32).astype(jnp.bfloat16)


def on_device(
    constraint_features,
    variable_features,
    variable_cotangent,
    constraint_weight,
    variable_weight,
    bias,
    send_rows,
    recv_count,
    edge_slots,
):
    device_count = lax.axis_size(DEVICE_AXES)
    slot_cap = send_rows.shape[2] // device_count
    embedding_width = constraint_features.shape[1]
    replica_rows = device_count * slot_cap
    master_rows = constraint_features.shape[0]
    select_con = one_hot_table(send_rows[0, 0], master_rows)
    select_var = one_hot_table(send_rows[1, 0], master_rows)
    out_con = pick_rows(select_con, constraint_features)
    out_var = pick_rows(select_var, variable_features)
    out_cot = pick_rows(select_var, variable_cotangent)
    outgoing = jnp.concatenate([out_con, out_var, out_cot], axis=1).reshape(
        device_count, slot_cap, 3 * embedding_width
    )
    incoming = lax.all_to_all(outgoing, DEVICE_AXES, split_axis=0, concat_axis=0, tiled=True)
    constraint_mirror_rows = incoming[:, :, :embedding_width]
    variable_mirror_rows = incoming[:, :, embedding_width : 2 * embedding_width]
    cotangent_mirror_rows = incoming[:, :, 2 * embedding_width :]
    slot_pos = lax.broadcasted_iota(jnp.int32, (2, replica_rows), 1) % slot_cap
    slot_live = jnp.where(
        slot_pos < jnp.repeat(recv_count[:, 0], slot_cap, axis=1), 1.0, 0.0
    ).astype(jnp.bfloat16)
    table_con = one_hot_table(edge_slots[0], replica_rows)
    table_var = one_hot_table(edge_slots[1], replica_rows)
    live_con = jnp.dot(table_con, slot_live[0], preferred_element_type=jnp.float32)
    live_var = jnp.dot(table_var, slot_live[1], preferred_element_type=jnp.float32)
    edge_active_mask = live_con * live_var
    slot_dims = (((1, 2), (0, 1)), ((), ()))
    table_con3 = table_con.reshape(-1, device_count, slot_cap)
    table_var3 = table_var.reshape(-1, device_count, slot_cap)
    edge_con = lax.dot_general(
        table_con3, constraint_mirror_rows, slot_dims, preferred_element_type=jnp.float32
    ).astype(jnp.bfloat16)
    edge_var = lax.dot_general(
        table_var3, variable_mirror_rows, slot_dims, preferred_element_type=jnp.float32
    ).astype(jnp.bfloat16)
    upstream_gradient = lax.dot_general(
        table_var3, cotangent_mirror_rows, slot_dims, preferred_element_type=jnp.float32
    )
    pre_act = (
        jnp.dot(edge_con, constraint_weight, preferred_element_type=jnp.float32)
        + jnp.dot(edge_var, variable_weight, preferred_element_type=jnp.float32)
        + bias[None, :]
    )
    sigmoid_pre = jax.nn.sigmoid(pre_act)
    message_derivative = sigmoid_pre * (1.0 + pre_act * (1.0 - sigmoid_pre))
    edge_delta = (upstream_gradient * message_derivative * edge_active_mask[:, None]).astype(
        jnp.bfloat16
    )
    sum_dims = (((0,), (0,)), ((), ()))
    constraint_projection_gradient = lax.dot_general(
        table_con, edge_delta, sum_dims, preferred_element_type=jnp.float32
    ).astype(jnp.bfloat16)
    variable_projection_gradient = lax.dot_general(
        table_var, edge_delta, sum_dims, preferred_element_type=jnp.float32
    ).astype(jnp.bfloat16)
    back_con = jnp.dot(
        constraint_projection_gradient, constraint_weight.T, preferred_element_type=jnp.float32
    ).astype(jnp.bfloat16)
    back_var = jnp.dot(
        variable_projection_gradient, variable_weight.T, preferred_element_type=jnp.float32
    ).astype(jnp.bfloat16)
    backward = jnp.concatenate([back_con, back_var], axis=1).reshape(
        device_count, slot_cap, 2 * embedding_width
    )
    constraint_term = lax.dot_general(
        constraint_mirror_rows,
        constraint_projection_gradient.reshape(device_count, slot_cap, embedding_width),
        (((0, 1), (0, 1)), ((), ())),
        preferred_element_type=jnp.float32,
    )
    variable_term = lax.dot_general(
        variable_mirror_rows,
        variable_projection_gradient.reshape(device_count, slot_cap, embedding_width),
        (((0, 1), (0, 1)), ((), ())),
        preferred_element_type=jnp.float32,
    )
    term_bias = jnp.sum(edge_delta.astype(jnp.float32), axis=0)
    factor = float(device_count * edge_slots.shape[1]) ** (-0.5)
    share = embedding_width // device_count
    lanes = 128
    bias_rows = jnp.pad(
        term_bias.reshape(device_count, 1, share), ((0, 0), (0, 7), (0, lanes - share))
    )
    partials = jnp.concatenate(
        [
            constraint_term.reshape(device_count, -1, lanes),
            variable_term.reshape(device_count, -1, lanes),
            bias_rows,
        ],
        axis=1,
    )
    summed = partials.reshape(*(lax.axis_size(name) for name in DEVICE_AXES), -1, lanes)
    for axis_name, position in (("c", 1), ("x", 3), ("z", 2), ("y", 0)):
        if axis_name == "x":
            backward, summed = lax.optimization_barrier((backward, summed))
            homes = lax.all_to_all(backward, DEVICE_AXES, split_axis=0, concat_axis=0, tiled=True)
            home_con = homes[:, :, :embedding_width]
            home_var = homes[:, :, embedding_width:]
        ring = lax.axis_size(axis_name)
        me = lax.axis_index(axis_name)
        sent = summed.astype(jnp.bfloat16)
        total = lax.dynamic_slice_in_dim(summed, me, 1, position)
        for shift in range(1, ring):
            chunk = lax.dynamic_slice_in_dim(sent, (me + shift) % ring, 1, position)
            pairs = [(i, (i + shift) % ring) for i in range(ring)]
            total = total + lax.ppermute(chunk, axis_name, pairs).astype(jnp.float32)
        summed = total
    summed = summed.reshape(-1, lanes)
    grad_con = lax.dot_general(
        select_con.reshape(device_count, slot_cap, -1),
        home_con,
        (((0, 1), (0, 1)), ((), ())),
        preferred_element_type=jnp.float32,
    )
    grad_var = lax.dot_general(
        select_var.reshape(device_count, slot_cap, -1),
        home_var,
        (((0, 1), (0, 1)), ((), ())),
        preferred_element_type=jnp.float32,
    )
    grad_var = variable_cotangent.astype(jnp.float32) + grad_var
    term_rows = share * embedding_width // lanes
    sum_con = summed[:term_rows].reshape(share, embedding_width)
    sum_var = summed[term_rows : 2 * term_rows].reshape(share, embedding_width)
    sum_bias = summed[2 * term_rows, :share]
    return (
        grad_con.astype(jnp.bfloat16),
        grad_var.astype(jnp.bfloat16),
        sum_con * factor,
        sum_var * factor,
        sum_bias * factor,
    )


def solution(mesh):
    placed = (
        P(DEVICE_AXES, None),
        P(DEVICE_AXES, None),
        P(DEVICE_AXES, None),
        P(),
        P(),
        P(),
        P(None, DEVICE_AXES, None),
        P(None, DEVICE_AXES, None),
        P(None, DEVICE_AXES),
    )
    rows, cols = mesh.devices.shape
    torus = Mesh(mesh.devices.reshape(rows // 2, 2, cols // 4, 4), DEVICE_AXES)
    return jax.shard_map(
        on_device,
        mesh=torus,
        in_specs=placed,
        out_specs=(
            P(DEVICE_AXES, None),
            P(DEVICE_AXES, None),
            P(DEVICE_AXES, None),
            P(DEVICE_AXES, None),
            P(DEVICE_AXES),
        ),
        check_vma=False,
    )
```

```python
import jax
import jax.numpy as jnp
from jax import lax
from jax.sharding import Mesh, PartitionSpec as P

DEVICE_AXES = ("y", "c", "z", "x")


def one_hot_table(indices, width):
    columns = lax.broadcasted_iota(jnp.int32, (indices.shape[0], width), 1)
    return jnp.where(columns == indices[:, None], 1.0, 0.0).astype(jnp.bfloat16)


def pick_rows(table, values):
    return jnp.dot(table, values, preferred_element_type=jnp.float32).astype(jnp.bfloat16)


def on_device(
    constraint_features,
    variable_features,
    variable_cotangent,
    constraint_weight,
    variable_weight,
    bias,
    send_rows,
    recv_count,
    edge_slots,
):
    device_count = lax.axis_size(DEVICE_AXES)
    slot_cap = send_rows.shape[2] // device_count
    embedding_width = constraint_features.shape[1]
    replica_rows = device_count * slot_cap
    master_rows = constraint_features.shape[0]
    select_con = one_hot_table(send_rows[0, 0], master_rows)
    select_var = one_hot_table(send_rows[1, 0], master_rows)
    out_con = pick_rows(select_con, constraint_features)
    out_var = pick_rows(select_var, variable_features)
    out_cot = pick_rows(select_var, variable_cotangent)
    outgoing = jnp.concatenate([out_con, out_var, out_cot], axis=1).reshape(
        device_count, slot_cap, 3 * embedding_width
    )
    incoming = lax.all_to_all(outgoing, DEVICE_AXES, split_axis=0, concat_axis=0, tiled=True)
    constraint_mirror_rows = incoming[:, :, :embedding_width]
    variable_mirror_rows = incoming[:, :, embedding_width : 2 * embedding_width]
    cotangent_mirror_rows = incoming[:, :, 2 * embedding_width :]
    slot_pos = lax.broadcasted_iota(jnp.int32, (2, replica_rows), 1) % slot_cap
    slot_live = jnp.where(
        slot_pos < jnp.repeat(recv_count[:, 0], slot_cap, axis=1), 1.0, 0.0
    ).astype(jnp.bfloat16)
    table_con = one_hot_table(edge_slots[0], replica_rows)
    table_var = one_hot_table(edge_slots[1], replica_rows)
    live_con = jnp.dot(table_con, slot_live[0], preferred_element_type=jnp.float32)
    live_var = jnp.dot(table_var, slot_live[1], preferred_element_type=jnp.float32)
    edge_active_mask = live_con * live_var
    slot_dims = (((1, 2), (0, 1)), ((), ()))
    table_con3 = table_con.reshape(-1, device_count, slot_cap)
    table_var3 = table_var.reshape(-1, device_count, slot_cap)
    edge_con = lax.dot_general(
        table_con3, constraint_mirror_rows, slot_dims, preferred_element_type=jnp.float32
    ).astype(jnp.bfloat16)
    edge_var = lax.dot_general(
        table_var3, variable_mirror_rows, slot_dims, preferred_element_type=jnp.float32
    ).astype(jnp.bfloat16)
    upstream_gradient = lax.dot_general(
        table_var3, cotangent_mirror_rows, slot_dims, preferred_element_type=jnp.float32
    )
    pre_act = (
        jnp.dot(edge_con, constraint_weight, preferred_element_type=jnp.float32)
        + jnp.dot(edge_var, variable_weight, preferred_element_type=jnp.float32)
        + bias[None, :]
    )
    sigmoid_pre = jax.nn.sigmoid(pre_act)
    message_derivative = sigmoid_pre * (1.0 + pre_act * (1.0 - sigmoid_pre))
    edge_delta = (upstream_gradient * message_derivative * edge_active_mask[:, None]).astype(
        jnp.bfloat16
    )
    sum_dims = (((0,), (0,)), ((), ()))
    constraint_projection_gradient = lax.dot_general(
        table_con3, edge_delta, sum_dims, preferred_element_type=jnp.float32
    ).astype(jnp.bfloat16)
    variable_projection_gradient = lax.dot_general(
        table_var3, edge_delta, sum_dims, preferred_element_type=jnp.float32
    ).astype(jnp.bfloat16)
    back_con = jnp.dot(
        constraint_projection_gradient, constraint_weight.T, preferred_element_type=jnp.float32
    ).astype(jnp.bfloat16)
    back_var = jnp.dot(
        variable_projection_gradient, variable_weight.T, preferred_element_type=jnp.float32
    ).astype(jnp.bfloat16)
    backward = jnp.concatenate([back_con, back_var], axis=2)
    constraint_term = lax.dot_general(
        constraint_mirror_rows,
        constraint_projection_gradient,
        (((0, 1), (0, 1)), ((), ())),
        preferred_element_type=jnp.float32,
    )
    variable_term = lax.dot_general(
        variable_mirror_rows,
        variable_projection_gradient,
        (((0, 1), (0, 1)), ((), ())),
        preferred_element_type=jnp.float32,
    )
    term_bias = jnp.sum(edge_delta.astype(jnp.float32), axis=0)
    factor = float(device_count * edge_slots.shape[1]) ** (-0.5)
    share = embedding_width // device_count
    lanes = 128
    bias_rows = jnp.pad(
        term_bias.reshape(device_count, 1, share), ((0, 0), (0, 7), (0, lanes - share))
    )
    partials = jnp.concatenate(
        [
            constraint_term.reshape(device_count, -1, lanes),
            variable_term.reshape(device_count, -1, lanes),
            bias_rows,
        ],
        axis=1,
    )
    summed = partials.reshape(*(lax.axis_size(name) for name in DEVICE_AXES), -1, lanes)
    for axis_name, position in (("c", 1), ("x", 3), ("z", 2), ("y", 0)):
        if axis_name == "x":
            backward, summed = lax.optimization_barrier((backward, summed))
            homes = lax.all_to_all(backward, DEVICE_AXES, split_axis=0, concat_axis=0, tiled=True)
            home_con = homes[:, :, :embedding_width]
            home_var = homes[:, :, embedding_width:]
        ring = lax.axis_size(axis_name)
        me = lax.axis_index(axis_name)
        sent = summed.astype(jnp.bfloat16)
        total = lax.dynamic_slice_in_dim(summed, me, 1, position)
        for shift in range(1, ring):
            chunk = lax.dynamic_slice_in_dim(sent, (me + shift) % ring, 1, position)
            pairs = [(i, (i + shift) % ring) for i in range(ring)]
            total = total + lax.ppermute(chunk, axis_name, pairs).astype(jnp.float32)
        summed = total
    summed = summed.reshape(-1, lanes)
    grad_con = lax.dot_general(
        select_con.reshape(device_count, slot_cap, -1),
        home_con,
        (((0, 1), (0, 1)), ((), ())),
        preferred_element_type=jnp.float32,
    )
    grad_var = lax.dot_general(
        select_var.reshape(device_count, slot_cap, -1),
        home_var,
        (((0, 1), (0, 1)), ((), ())),
        preferred_element_type=jnp.float32,
    )
    grad_var = variable_cotangent.astype(jnp.float32) + grad_var
    term_rows = share * embedding_width // lanes
    sum_con = summed[:term_rows].reshape(share, embedding_width)
    sum_var = summed[term_rows : 2 * term_rows].reshape(share, embedding_width)
    sum_bias = summed[2 * term_rows, :share]
    return (
        grad_con.astype(jnp.bfloat16),
        grad_var.astype(jnp.bfloat16),
        sum_con * factor,
        sum_var * factor,
        sum_bias * factor,
    )


def solution(mesh):
    placed = (
        P(DEVICE_AXES, None),
        P(DEVICE_AXES, None),
        P(DEVICE_AXES, None),
        P(),
        P(),
        P(),
        P(None, DEVICE_AXES, None),
        P(None, DEVICE_AXES, None),
        P(None, DEVICE_AXES),
    )
    rows, cols = mesh.devices.shape
    torus = Mesh(mesh.devices.reshape(rows // 2, 2, cols // 4, 4), DEVICE_AXES)
    return jax.shard_map(
        on_device,
        mesh=torus,
        in_specs=placed,
        out_specs=(
            P(DEVICE_AXES, None),
            P(DEVICE_AXES, None),
            P(DEVICE_AXES, None),
            P(DEVICE_AXES, None),
            P(DEVICE_AXES),
        ),
        check_vma=False,
    )
```

```python
import jax
import jax.numpy as jnp
from jax import lax
from jax.sharding import Mesh, PartitionSpec as P

DEVICE_AXES = ("y", "c", "z", "x")


def one_hot_table(indices, width):
    columns = lax.broadcasted_iota(jnp.int32, (indices.shape[0], width), 1)
    return jnp.where(columns == indices[:, None], 1.0, 0.0).astype(jnp.bfloat16)


def pick_rows(table, values):
    return jnp.dot(table, values, preferred_element_type=jnp.float32).astype(jnp.bfloat16)


def on_device(
    constraint_features,
    variable_features,
    variable_cotangent,
    constraint_weight,
    variable_weight,
    bias,
    send_rows,
    recv_count,
    edge_slots,
):
    device_count = lax.axis_size(DEVICE_AXES)
    slot_cap = send_rows.shape[2] // device_count
    embedding_width = constraint_features.shape[1]
    replica_rows = device_count * slot_cap
    master_rows = constraint_features.shape[0]
    slot_shape = (device_count, slot_cap, master_rows)
    master_ids = lax.broadcasted_iota(jnp.int32, slot_shape, 2)
    select_con = jnp.where(
        master_ids == send_rows[0, 0].reshape(device_count, slot_cap, 1), 1.0, 0.0
    ).astype(jnp.bfloat16)
    select_var = jnp.where(
        master_ids == send_rows[1, 0].reshape(device_count, slot_cap, 1), 1.0, 0.0
    ).astype(jnp.bfloat16)
    out_con = pick_rows(select_con, constraint_features)
    out_var = pick_rows(select_var, variable_features)
    out_cot = pick_rows(select_var, variable_cotangent)
    outgoing = jnp.concatenate([out_con, out_var, out_cot], axis=2)
    incoming = lax.all_to_all(outgoing, DEVICE_AXES, split_axis=0, concat_axis=0, tiled=True)
    constraint_mirror_rows = incoming[:, :, :embedding_width]
    variable_mirror_rows = incoming[:, :, embedding_width : 2 * embedding_width]
    cotangent_mirror_rows = incoming[:, :, 2 * embedding_width :]
    slot_pos = lax.broadcasted_iota(jnp.int32, (2, replica_rows), 1) % slot_cap
    slot_live = jnp.where(
        slot_pos < jnp.repeat(recv_count[:, 0], slot_cap, axis=1), 1.0, 0.0
    ).astype(jnp.bfloat16)
    table_con = one_hot_table(edge_slots[0], replica_rows)
    table_var = one_hot_table(edge_slots[1], replica_rows)
    live_con = jnp.dot(table_con, slot_live[0], preferred_element_type=jnp.float32)
    live_var = jnp.dot(table_var, slot_live[1], preferred_element_type=jnp.float32)
    edge_active_mask = live_con * live_var
    slot_dims = (((1, 2), (0, 1)), ((), ()))
    table_con3 = table_con.reshape(-1, device_count, slot_cap)
    table_var3 = table_var.reshape(-1, device_count, slot_cap)
    edge_con = lax.dot_general(
        table_con3, constraint_mirror_rows, slot_dims, preferred_element_type=jnp.float32
    ).astype(jnp.bfloat16)
    edge_var = lax.dot_general(
        table_var3, variable_mirror_rows, slot_dims, preferred_element_type=jnp.float32
    ).astype(jnp.bfloat16)
    upstream_gradient = lax.dot_general(
        table_var3, cotangent_mirror_rows, slot_dims, preferred_element_type=jnp.float32
    )
    pre_act = (
        jnp.dot(edge_con, constraint_weight, preferred_element_type=jnp.float32)
        + jnp.dot(edge_var, variable_weight, preferred_element_type=jnp.float32)
        + bias[None, :]
    )
    sigmoid_pre = jax.nn.sigmoid(pre_act)
    message_derivative = sigmoid_pre * (1.0 + pre_act * (1.0 - sigmoid_pre))
    edge_delta = (upstream_gradient * message_derivative * edge_active_mask[:, None]).astype(
        jnp.bfloat16
    )
    sum_dims = (((0,), (0,)), ((), ()))
    constraint_projection_gradient = lax.dot_general(
        table_con3, edge_delta, sum_dims, preferred_element_type=jnp.float32
    ).astype(jnp.bfloat16)
    variable_projection_gradient = lax.dot_general(
        table_var3, edge_delta, sum_dims, preferred_element_type=jnp.float32
    ).astype(jnp.bfloat16)
    back_con = jnp.dot(
        constraint_projection_gradient, constraint_weight.T, preferred_element_type=jnp.float32
    ).astype(jnp.bfloat16)
    back_var = jnp.dot(
        variable_projection_gradient, variable_weight.T, preferred_element_type=jnp.float32
    ).astype(jnp.bfloat16)
    backward = jnp.concatenate([back_con, back_var], axis=2)
    constraint_term = lax.dot_general(
        constraint_mirror_rows,
        constraint_projection_gradient,
        (((0, 1), (0, 1)), ((), ())),
        preferred_element_type=jnp.float32,
    )
    variable_term = lax.dot_general(
        variable_mirror_rows,
        variable_projection_gradient,
        (((0, 1), (0, 1)), ((), ())),
        preferred_element_type=jnp.float32,
    )
    term_bias = jnp.sum(edge_delta.astype(jnp.float32), axis=0)
    factor = float(device_count * edge_slots.shape[1]) ** (-0.5)
    share = embedding_width // device_count
    lanes = 128
    bias_rows = jnp.pad(
        term_bias.reshape(device_count, 1, share), ((0, 0), (0, 7), (0, lanes - share))
    )
    partials = jnp.concatenate(
        [
            constraint_term.reshape(device_count, -1, lanes),
            variable_term.reshape(device_count, -1, lanes),
            bias_rows,
        ],
        axis=1,
    )
    summed = partials.reshape(*(lax.axis_size(name) for name in DEVICE_AXES), -1, lanes)
    for axis_name, position in (("c", 1), ("x", 3), ("z", 2), ("y", 0)):
        if axis_name == "x":
            backward, summed = lax.optimization_barrier((backward, summed))
            homes = lax.all_to_all(backward, DEVICE_AXES, split_axis=0, concat_axis=0, tiled=True)
            home_con = homes[:, :, :embedding_width]
            home_var = homes[:, :, embedding_width:]
        ring = lax.axis_size(axis_name)
        me = lax.axis_index(axis_name)
        sent = summed.astype(jnp.bfloat16)
        total = lax.dynamic_slice_in_dim(summed, me, 1, position)
        for shift in range(1, ring):
            chunk = lax.dynamic_slice_in_dim(sent, (me + shift) % ring, 1, position)
            pairs = [(i, (i + shift) % ring) for i in range(ring)]
            total = total + lax.ppermute(chunk, axis_name, pairs).astype(jnp.float32)
        summed = total
    summed = summed.reshape(-1, lanes)
    grad_con = lax.dot_general(
        select_con,
        home_con,
        (((0, 1), (0, 1)), ((), ())),
        preferred_element_type=jnp.float32,
    )
    grad_var = lax.dot_general(
        select_var,
        home_var,
        (((0, 1), (0, 1)), ((), ())),
        preferred_element_type=jnp.float32,
    )
    grad_var = variable_cotangent.astype(jnp.float32) + grad_var
    term_rows = share * embedding_width // lanes
    sum_con = summed[:term_rows].reshape(share, embedding_width)
    sum_var = summed[term_rows : 2 * term_rows].reshape(share, embedding_width)
    sum_bias = summed[2 * term_rows, :share]
    return (
        grad_con.astype(jnp.bfloat16),
        grad_var.astype(jnp.bfloat16),
        sum_con * factor,
        sum_var * factor,
        sum_bias * factor,
    )


def solution(mesh):
    placed = (
        P(DEVICE_AXES, None),
        P(DEVICE_AXES, None),
        P(DEVICE_AXES, None),
        P(),
        P(),
        P(),
        P(None, DEVICE_AXES, None),
        P(None, DEVICE_AXES, None),
        P(None, DEVICE_AXES),
    )
    rows, cols = mesh.devices.shape
    torus = Mesh(mesh.devices.reshape(rows // 2, 2, cols // 4, 4), DEVICE_AXES)
    return jax.shard_map(
        on_device,
        mesh=torus,
        in_specs=placed,
        out_specs=(
            P(DEVICE_AXES, None),
            P(DEVICE_AXES, None),
            P(DEVICE_AXES, None),
            P(DEVICE_AXES, None),
            P(DEVICE_AXES),
        ),
        check_vma=False,
    )
```

```python
import jax
import jax.numpy as jnp
from jax import lax
from jax.sharding import Mesh, PartitionSpec as P

DEVICE_AXES = ("y", "c", "z", "x")


def one_hot_table(indices, width):
    columns = lax.broadcasted_iota(jnp.int32, (indices.shape[0], width), 1)
    return jnp.where(columns == indices[:, None], 1.0, 0.0).astype(jnp.bfloat16)


def pick_rows(table, values):
    return jnp.dot(table, values, preferred_element_type=jnp.float32).astype(jnp.bfloat16)


def on_device(
    constraint_features,
    variable_features,
    variable_cotangent,
    constraint_weight,
    variable_weight,
    bias,
    send_rows,
    recv_count,
    edge_slots,
):
    device_count = lax.axis_size(DEVICE_AXES)
    slot_cap = send_rows.shape[2] // device_count
    embedding_width = constraint_features.shape[1]
    replica_rows = device_count * slot_cap
    master_rows = constraint_features.shape[0]
    select_con = one_hot_table(send_rows[0, 0], master_rows)
    select_var = one_hot_table(send_rows[1, 0], master_rows)
    out_con = pick_rows(select_con, constraint_features)
    out_var = pick_rows(select_var, variable_features)
    out_cot = pick_rows(select_var, variable_cotangent)
    outgoing = jnp.concatenate([out_con, out_var, out_cot], axis=1).reshape(
        device_count, slot_cap, 3 * embedding_width
    )
    incoming = lax.all_to_all(outgoing, DEVICE_AXES, split_axis=0, concat_axis=0, tiled=True)
    constraint_mirror_rows = incoming[:, :, :embedding_width]
    variable_mirror_rows = incoming[:, :, embedding_width : 2 * embedding_width]
    cotangent_mirror_rows = incoming[:, :, 2 * embedding_width :]
    slot_pos = lax.broadcasted_iota(jnp.int32, (2, replica_rows), 1) % slot_cap
    slot_live = jnp.where(
        slot_pos < jnp.repeat(recv_count[:, 0], slot_cap, axis=1), 1.0, 0.0
    ).astype(jnp.bfloat16)
    table_con = one_hot_table(edge_slots[0], replica_rows)
    table_var = one_hot_table(edge_slots[1], replica_rows)
    live_con = jnp.dot(table_con, slot_live[0], preferred_element_type=jnp.float32)
    live_var = jnp.dot(table_var, slot_live[1], preferred_element_type=jnp.float32)
    edge_active_mask = live_con * live_var
    slot_dims = (((1, 2), (0, 1)), ((), ()))
    table_con3 = table_con.reshape(-1, device_count, slot_cap)
    table_var3 = table_var.reshape(-1, device_count, slot_cap)
    edge_con = lax.dot_general(
        table_con3, constraint_mirror_rows, slot_dims, preferred_element_type=jnp.float32
    ).astype(jnp.bfloat16)
    edge_var = lax.dot_general(
        table_var3, variable_mirror_rows, slot_dims, preferred_element_type=jnp.float32
    ).astype(jnp.bfloat16)
    upstream_gradient = lax.dot_general(
        table_var3, cotangent_mirror_rows, slot_dims, preferred_element_type=jnp.float32
    )
    pre_act = (
        jnp.dot(edge_con, constraint_weight, preferred_element_type=jnp.float32)
        + jnp.dot(edge_var, variable_weight, preferred_element_type=jnp.float32)
        + bias[None, :]
    )
    sigmoid_pre = jax.nn.sigmoid(pre_act)
    message_derivative = sigmoid_pre * (1.0 + pre_act * (1.0 - sigmoid_pre))
    edge_delta = (upstream_gradient * message_derivative * edge_active_mask[:, None]).astype(
        jnp.bfloat16
    )
    sum_dims = (((0,), (0,)), ((), ()))
    constraint_projection_gradient = lax.dot_general(
        table_con3, edge_delta, sum_dims, preferred_element_type=jnp.float32
    ).astype(jnp.bfloat16)
    variable_projection_gradient = lax.dot_general(
        table_var3, edge_delta, sum_dims, preferred_element_type=jnp.float32
    ).astype(jnp.bfloat16)
    back_con = jnp.dot(
        constraint_projection_gradient, constraint_weight.T, preferred_element_type=jnp.float32
    ).astype(jnp.bfloat16)
    back_var = jnp.dot(
        variable_projection_gradient, variable_weight.T, preferred_element_type=jnp.float32
    ).astype(jnp.bfloat16)
    backward = jnp.concatenate([back_con, back_var], axis=2)
    constraint_term = lax.dot_general(
        constraint_mirror_rows,
        constraint_projection_gradient,
        (((0, 1), (0, 1)), ((), ())),
        preferred_element_type=jnp.float32,
    )
    variable_term = lax.dot_general(
        variable_mirror_rows,
        variable_projection_gradient,
        (((0, 1), (0, 1)), ((), ())),
        preferred_element_type=jnp.float32,
    )
    term_bias = jnp.sum(edge_delta.astype(jnp.float32), axis=0)
    factor = float(device_count * edge_slots.shape[1]) ** (-0.5)
    share = embedding_width // device_count
    lanes = 128
    bias_rows = jnp.pad(
        term_bias.reshape(device_count, 1, share), ((0, 0), (0, 7), (0, lanes - share))
    )
    partials = jnp.concatenate(
        [
            constraint_term.astype(jnp.bfloat16).reshape(device_count, -1, lanes),
            variable_term.astype(jnp.bfloat16).reshape(device_count, -1, lanes),
            bias_rows.astype(jnp.bfloat16),
        ],
        axis=1,
    )
    summed = partials.reshape(*(lax.axis_size(name) for name in DEVICE_AXES), -1, lanes)
    for axis_name, position in (("c", 1), ("x", 3), ("z", 2), ("y", 0)):
        if axis_name == "x":
            backward, summed = lax.optimization_barrier((backward, summed))
            homes = lax.all_to_all(backward, DEVICE_AXES, split_axis=0, concat_axis=0, tiled=True)
            home_con = homes[:, :, :embedding_width]
            home_var = homes[:, :, embedding_width:]
        ring = lax.axis_size(axis_name)
        me = lax.axis_index(axis_name)
        sent = summed.astype(jnp.bfloat16)
        total = lax.dynamic_slice_in_dim(summed, me, 1, position).astype(jnp.float32)
        for shift in range(1, ring):
            chunk = lax.dynamic_slice_in_dim(sent, (me + shift) % ring, 1, position)
            pairs = [(i, (i + shift) % ring) for i in range(ring)]
            total = total + lax.ppermute(chunk, axis_name, pairs).astype(jnp.float32)
        summed = total
    summed = summed.reshape(-1, lanes)
    grad_con = lax.dot_general(
        select_con.reshape(device_count, slot_cap, -1),
        home_con,
        (((0, 1), (0, 1)), ((), ())),
        preferred_element_type=jnp.float32,
    )
    grad_var = lax.dot_general(
        select_var.reshape(device_count, slot_cap, -1),
        home_var,
        (((0, 1), (0, 1)), ((), ())),
        preferred_element_type=jnp.float32,
    )
    grad_var = variable_cotangent.astype(jnp.float32) + grad_var
    term_rows = share * embedding_width // lanes
    sum_con = summed[:term_rows].reshape(share, embedding_width)
    sum_var = summed[term_rows : 2 * term_rows].reshape(share, embedding_width)
    sum_bias = summed[2 * term_rows, :share]
    return (
        grad_con.astype(jnp.bfloat16),
        grad_var.astype(jnp.bfloat16),
        sum_con * factor,
        sum_var * factor,
        sum_bias * factor,
    )


def solution(mesh):
    placed = (
        P(DEVICE_AXES, None),
        P(DEVICE_AXES, None),
        P(DEVICE_AXES, None),
        P(),
        P(),
        P(),
        P(None, DEVICE_AXES, None),
        P(None, DEVICE_AXES, None),
        P(None, DEVICE_AXES),
    )
    rows, cols = mesh.devices.shape
    torus = Mesh(mesh.devices.reshape(rows // 2, 2, cols // 4, 4), DEVICE_AXES)
    return jax.shard_map(
        on_device,
        mesh=torus,
        in_specs=placed,
        out_specs=(
            P(DEVICE_AXES, None),
            P(DEVICE_AXES, None),
            P(DEVICE_AXES, None),
            P(DEVICE_AXES, None),
            P(DEVICE_AXES),
        ),
        check_vma=False,
    )
```

```python
import jax
import jax.numpy as jnp
from jax import lax
from jax.sharding import Mesh, PartitionSpec as P

DEVICE_AXES = ("y", "c", "z", "x")


def one_hot_table(indices, width):
    columns = lax.broadcasted_iota(jnp.int32, (indices.shape[0], width), 1)
    return jnp.where(columns == indices[:, None], 1.0, 0.0).astype(jnp.bfloat16)


def pick_rows(table, values):
    return jnp.dot(table, values, preferred_element_type=jnp.float32).astype(jnp.bfloat16)


def on_device(
    constraint_features,
    variable_features,
    variable_cotangent,
    constraint_weight,
    variable_weight,
    bias,
    send_rows,
    recv_count,
    edge_slots,
):
    device_count = lax.axis_size(DEVICE_AXES)
    slot_cap = send_rows.shape[2] // device_count
    embedding_width = constraint_features.shape[1]
    replica_rows = device_count * slot_cap
    master_rows = constraint_features.shape[0]
    select_con = one_hot_table(send_rows[0, 0], master_rows)
    select_var = one_hot_table(send_rows[1, 0], master_rows)
    out_con = pick_rows(select_con, constraint_features)
    out_var_cot = pick_rows(
        select_var, jnp.concatenate([variable_features, variable_cotangent], axis=1)
    )
    outgoing = jnp.concatenate([out_con, out_var_cot], axis=1).reshape(
        device_count, slot_cap, 3 * embedding_width
    )
    incoming = lax.all_to_all(outgoing, DEVICE_AXES, split_axis=0, concat_axis=0, tiled=True)
    constraint_mirror_rows = incoming[:, :, :embedding_width]
    variable_mirror_rows = incoming[:, :, embedding_width : 2 * embedding_width]
    cotangent_mirror_rows = incoming[:, :, 2 * embedding_width :]
    slot_pos = lax.broadcasted_iota(jnp.int32, (2, replica_rows), 1) % slot_cap
    slot_live = jnp.where(
        slot_pos < jnp.repeat(recv_count[:, 0], slot_cap, axis=1), 1.0, 0.0
    ).astype(jnp.bfloat16)
    table_con = one_hot_table(edge_slots[0], replica_rows)
    table_var = one_hot_table(edge_slots[1], replica_rows)
    live_con = jnp.dot(table_con, slot_live[0], preferred_element_type=jnp.float32)
    live_var = jnp.dot(table_var, slot_live[1], preferred_element_type=jnp.float32)
    edge_active_mask = live_con * live_var
    slot_dims = (((1, 2), (0, 1)), ((), ()))
    table_con3 = table_con.reshape(-1, device_count, slot_cap)
    table_var3 = table_var.reshape(-1, device_count, slot_cap)
    edge_con = lax.dot_general(
        table_con3, constraint_mirror_rows, slot_dims, preferred_element_type=jnp.float32
    ).astype(jnp.bfloat16)
    edge_var = lax.dot_general(
        table_var3, variable_mirror_rows, slot_dims, preferred_element_type=jnp.float32
    ).astype(jnp.bfloat16)
    upstream_gradient = lax.dot_general(
        table_var3, cotangent_mirror_rows, slot_dims, preferred_element_type=jnp.float32
    )
    pre_act = (
        jnp.dot(edge_con, constraint_weight, preferred_element_type=jnp.float32)
        + jnp.dot(edge_var, variable_weight, preferred_element_type=jnp.float32)
        + bias[None, :]
    )
    sigmoid_pre = jax.nn.sigmoid(pre_act)
    message_derivative = sigmoid_pre * (1.0 + pre_act * (1.0 - sigmoid_pre))
    edge_delta = (upstream_gradient * message_derivative * edge_active_mask[:, None]).astype(
        jnp.bfloat16
    )
    sum_dims = (((0,), (0,)), ((), ()))
    constraint_projection_gradient = lax.dot_general(
        table_con3, edge_delta, sum_dims, preferred_element_type=jnp.float32
    ).astype(jnp.bfloat16)
    variable_projection_gradient = lax.dot_general(
        table_var3, edge_delta, sum_dims, preferred_element_type=jnp.float32
    ).astype(jnp.bfloat16)
    back_con = jnp.dot(
        constraint_projection_gradient, constraint_weight.T, preferred_element_type=jnp.float32
    ).astype(jnp.bfloat16)
    back_var = jnp.dot(
        variable_projection_gradient, variable_weight.T, preferred_element_type=jnp.float32
    ).astype(jnp.bfloat16)
    backward = jnp.concatenate([back_con, back_var], axis=2)
    constraint_term = lax.dot_general(
        constraint_mirror_rows,
        constraint_projection_gradient,
        (((0, 1), (0, 1)), ((), ())),
        preferred_element_type=jnp.float32,
    )
    variable_term = lax.dot_general(
        variable_mirror_rows,
        variable_projection_gradient,
        (((0, 1), (0, 1)), ((), ())),
        preferred_element_type=jnp.float32,
    )
    term_bias = jnp.sum(edge_delta.astype(jnp.float32), axis=0)
    factor = float(device_count * edge_slots.shape[1]) ** (-0.5)
    share = embedding_width // device_count
    lanes = 128
    bias_rows = jnp.pad(
        term_bias.reshape(device_count, 1, share), ((0, 0), (0, 7), (0, lanes - share))
    )
    partials = jnp.concatenate(
        [
            constraint_term.reshape(device_count, -1, lanes),
            variable_term.reshape(device_count, -1, lanes),
            bias_rows,
        ],
        axis=1,
    )
    summed = partials.reshape(*(lax.axis_size(name) for name in DEVICE_AXES), -1, lanes)
    for axis_name, position in (("c", 1), ("x", 3), ("z", 2), ("y", 0)):
        if axis_name == "x":
            backward, summed = lax.optimization_barrier((backward, summed))
            homes = lax.all_to_all(backward, DEVICE_AXES, split_axis=0, concat_axis=0, tiled=True)
            home_con = homes[:, :, :embedding_width]
            home_var = homes[:, :, embedding_width:]
        ring = lax.axis_size(axis_name)
        me = lax.axis_index(axis_name)
        sent = summed.astype(jnp.bfloat16)
        total = lax.dynamic_slice_in_dim(summed, me, 1, position)
        for shift in range(1, ring):
            chunk = lax.dynamic_slice_in_dim(sent, (me + shift) % ring, 1, position)
            pairs = [(i, (i + shift) % ring) for i in range(ring)]
            total = total + lax.ppermute(chunk, axis_name, pairs).astype(jnp.float32)
        summed = total
    summed = summed.reshape(-1, lanes)
    grad_con = lax.dot_general(
        select_con.reshape(device_count, slot_cap, -1),
        home_con,
        (((0, 1), (0, 1)), ((), ())),
        preferred_element_type=jnp.float32,
    )
    grad_var = lax.dot_general(
        select_var.reshape(device_count, slot_cap, -1),
        home_var,
        (((0, 1), (0, 1)), ((), ())),
        preferred_element_type=jnp.float32,
    )
    grad_var = variable_cotangent.astype(jnp.float32) + grad_var
    term_rows = share * embedding_width // lanes
    sum_con = summed[:term_rows].reshape(share, embedding_width)
    sum_var = summed[term_rows : 2 * term_rows].reshape(share, embedding_width)
    sum_bias = summed[2 * term_rows, :share]
    return (
        grad_con.astype(jnp.bfloat16),
        grad_var.astype(jnp.bfloat16),
        sum_con * factor,
        sum_var * factor,
        sum_bias * factor,
    )


def solution(mesh):
    placed = (
        P(DEVICE_AXES, None),
        P(DEVICE_AXES, None),
        P(DEVICE_AXES, None),
        P(),
        P(),
        P(),
        P(None, DEVICE_AXES, None),
        P(None, DEVICE_AXES, None),
        P(None, DEVICE_AXES),
    )
    rows, cols = mesh.devices.shape
    torus = Mesh(mesh.devices.reshape(rows // 2, 2, cols // 4, 4), DEVICE_AXES)
    return jax.shard_map(
        on_device,
        mesh=torus,
        in_specs=placed,
        out_specs=(
            P(DEVICE_AXES, None),
            P(DEVICE_AXES, None),
            P(DEVICE_AXES, None),
            P(DEVICE_AXES, None),
            P(DEVICE_AXES),
        ),
        check_vma=False,
    )
```

```python
import jax
import jax.numpy as jnp
from jax import lax
from jax.sharding import Mesh, PartitionSpec as P

DEVICE_AXES = ("y", "c", "z", "x")


def one_hot_table(indices, width):
    columns = lax.broadcasted_iota(jnp.int32, (indices.shape[0], width), 1)
    return jnp.where(columns == indices[:, None], 1.0, 0.0).astype(jnp.bfloat16)


def pick_rows(table, values):
    return jnp.dot(table, values, preferred_element_type=jnp.float32).astype(jnp.bfloat16)


def on_device(
    constraint_features,
    variable_features,
    variable_cotangent,
    constraint_weight,
    variable_weight,
    bias,
    send_rows,
    recv_count,
    edge_slots,
):
    device_count = lax.axis_size(DEVICE_AXES)
    slot_cap = send_rows.shape[2] // device_count
    embedding_width = constraint_features.shape[1]
    replica_rows = device_count * slot_cap
    master_rows = constraint_features.shape[0]
    select_con = one_hot_table(send_rows[0, 0], master_rows)
    select_var = one_hot_table(send_rows[1, 0], master_rows)
    out_con = pick_rows(select_con, constraint_features)
    out_var_cot = pick_rows(
        select_var, jnp.concatenate([variable_features, variable_cotangent], axis=1)
    )
    outgoing = jnp.concatenate([out_con, out_var_cot], axis=1).reshape(
        device_count, slot_cap, 3 * embedding_width
    )
    incoming = lax.all_to_all(outgoing, DEVICE_AXES, split_axis=0, concat_axis=0, tiled=True)
    constraint_mirror_rows = incoming[:, :, :embedding_width]
    variable_mirror_rows = incoming[:, :, embedding_width : 2 * embedding_width]
    cotangent_mirror_rows = incoming[:, :, 2 * embedding_width :]
    slot_pos = lax.broadcasted_iota(jnp.int32, (2, replica_rows), 1) % slot_cap
    slot_live = jnp.where(
        slot_pos < jnp.repeat(recv_count[:, 0], slot_cap, axis=1), 1.0, 0.0
    ).astype(jnp.bfloat16)
    table_con = one_hot_table(edge_slots[0], replica_rows)
    table_var = one_hot_table(edge_slots[1], replica_rows)
    live_con = jnp.dot(table_con, slot_live[0], preferred_element_type=jnp.float32)
    live_var = jnp.dot(table_var, slot_live[1], preferred_element_type=jnp.float32)
    edge_active_mask = live_con * live_var
    slot_dims = (((1, 2), (0, 1)), ((), ()))
    table_con3 = table_con.reshape(-1, device_count, slot_cap)
    table_var3 = table_var.reshape(-1, device_count, slot_cap)
    edge_con = lax.dot_general(
        table_con3, constraint_mirror_rows, slot_dims, preferred_element_type=jnp.float32
    ).astype(jnp.bfloat16)
    edge_var = lax.dot_general(
        table_var3, variable_mirror_rows, slot_dims, preferred_element_type=jnp.float32
    ).astype(jnp.bfloat16)
    upstream_gradient = lax.dot_general(
        table_var3, cotangent_mirror_rows, slot_dims, preferred_element_type=jnp.float32
    )
    pre_act = (
        jnp.dot(edge_con, constraint_weight, preferred_element_type=jnp.float32)
        + jnp.dot(edge_var, variable_weight, preferred_element_type=jnp.float32)
        + bias[None, :]
    )
    sigmoid_pre = jax.nn.sigmoid(pre_act)
    message_derivative = sigmoid_pre * (1.0 + pre_act * (1.0 - sigmoid_pre))
    edge_delta = (upstream_gradient * message_derivative * edge_active_mask[:, None]).astype(
        jnp.bfloat16
    )
    sum_dims = (((0,), (0,)), ((), ()))
    constraint_projection_gradient = lax.dot_general(
        table_con3, edge_delta, sum_dims, preferred_element_type=jnp.float32
    ).astype(jnp.bfloat16)
    variable_projection_gradient = lax.dot_general(
        table_var3, edge_delta, sum_dims, preferred_element_type=jnp.float32
    ).astype(jnp.bfloat16)
    back_con = jnp.dot(
        constraint_projection_gradient, constraint_weight.T, preferred_element_type=jnp.float32
    ).astype(jnp.bfloat16)
    back_var = jnp.dot(
        variable_projection_gradient, variable_weight.T, preferred_element_type=jnp.float32
    ).astype(jnp.bfloat16)
    backward = jnp.concatenate([back_con, back_var], axis=2)
    constraint_term = lax.dot_general(
        constraint_mirror_rows,
        constraint_projection_gradient,
        (((0, 1), (0, 1)), ((), ())),
        preferred_element_type=jnp.float32,
    )
    variable_term = lax.dot_general(
        variable_mirror_rows,
        variable_projection_gradient,
        (((0, 1), (0, 1)), ((), ())),
        preferred_element_type=jnp.float32,
    )
    term_bias = jnp.sum(edge_delta.astype(jnp.float32), axis=0)
    factor = float(device_count * edge_slots.shape[1]) ** (-0.5)
    share = embedding_width // device_count
    lanes = 128
    bias_rows = jnp.pad(
        term_bias.reshape(device_count, 1, share), ((0, 0), (0, 7), (0, lanes - share))
    )
    partials = jnp.concatenate(
        [
            constraint_term.reshape(device_count, -1, lanes),
            variable_term.reshape(device_count, -1, lanes),
            bias_rows,
        ],
        axis=1,
    )
    summed = partials.reshape(*(lax.axis_size(name) for name in DEVICE_AXES), -1, lanes)
    for axis_name, position in (("c", 1), ("x", 3), ("z", 2), ("y", 0)):
        if axis_name == "z":
            backward, summed = lax.optimization_barrier((backward, summed))
            homes = lax.all_to_all(backward, DEVICE_AXES, split_axis=0, concat_axis=0, tiled=True)
            home_con = homes[:, :, :embedding_width]
            home_var = homes[:, :, embedding_width:]
        ring = lax.axis_size(axis_name)
        me = lax.axis_index(axis_name)
        sent = summed.astype(jnp.bfloat16)
        total = lax.dynamic_slice_in_dim(summed, me, 1, position)
        for shift in range(1, ring):
            chunk = lax.dynamic_slice_in_dim(sent, (me + shift) % ring, 1, position)
            pairs = [(i, (i + shift) % ring) for i in range(ring)]
            total = total + lax.ppermute(chunk, axis_name, pairs).astype(jnp.float32)
        summed = total
    summed = summed.reshape(-1, lanes)
    grad_con = lax.dot_general(
        select_con.reshape(device_count, slot_cap, -1),
        home_con,
        (((0, 1), (0, 1)), ((), ())),
        preferred_element_type=jnp.float32,
    )
    grad_var = lax.dot_general(
        select_var.reshape(device_count, slot_cap, -1),
        home_var,
        (((0, 1), (0, 1)), ((), ())),
        preferred_element_type=jnp.float32,
    )
    grad_var = variable_cotangent.astype(jnp.float32) + grad_var
    term_rows = share * embedding_width // lanes
    sum_con = summed[:term_rows].reshape(share, embedding_width)
    sum_var = summed[term_rows : 2 * term_rows].reshape(share, embedding_width)
    sum_bias = summed[2 * term_rows, :share]
    return (
        grad_con.astype(jnp.bfloat16),
        grad_var.astype(jnp.bfloat16),
        sum_con * factor,
        sum_var * factor,
        sum_bias * factor,
    )


def solution(mesh):
    placed = (
        P(DEVICE_AXES, None),
        P(DEVICE_AXES, None),
        P(DEVICE_AXES, None),
        P(),
        P(),
        P(),
        P(None, DEVICE_AXES, None),
        P(None, DEVICE_AXES, None),
        P(None, DEVICE_AXES),
    )
    rows, cols = mesh.devices.shape
    torus = Mesh(mesh.devices.reshape(rows // 2, 2, cols // 4, 4), DEVICE_AXES)
    return jax.shard_map(
        on_device,
        mesh=torus,
        in_specs=placed,
        out_specs=(
            P(DEVICE_AXES, None),
            P(DEVICE_AXES, None),
            P(DEVICE_AXES, None),
            P(DEVICE_AXES, None),
            P(DEVICE_AXES),
        ),
        check_vma=False,
    )
```
